1024 devices in a mesh: outer: 16 (over z), inner: 64 (over x, y, core).
Axes of the slice: x: 4, y: 8, z: 16, core: 2. Of those that a mesh axis runs over, the one named last changes fastest.
Arguments:
- projected: bfloat16 [8192, 3, 4096], P('inner', None, 'outer'), may hold values from -6 to 6
- short_weight: float32 [7, 3, 4096], P(None, None, 'outer'), may hold values from -2.5 to 2.5
- filter_in: float32 [33, 64], replicated, may hold values from -1 to 1
- filter_bias: float32 [64], replicated, may hold values from -3.140625 to 3.140625
- filter_out: float32 [64, 4096], P(None, 'outer'), may hold values from -0.75 to 0.75
- filter_decay: float32 [4096], P('outer'), as said below
- cotangent: bfloat16 [8192, 4096], P('inner', 'outer'), may hold values from -6 to 6
Outputs:
- operator_out: bfloat16 [8192, 4096], P('inner', 'outer')
- grad_projected: bfloat16 [8192, 3, 4096], P('inner', None, 'outer')
- grad_filter: float32 [8192, 4096], P('inner', 'outer')
The draws below stay inside these ranges and needn't reach their ends.
Inputs may be any that keep to these rules, and one draw needn't show every extreme that they name: Every rate in filter_decay is positive, at least 0.3 / 8192 and at most 1 / 30.
All inputs are finite; a program needn't handle non-finite values.
Results may differ from the reference program's by a relative error of at most 0.00155.
Values may be sent and summed in bfloat16 or wider, within the bound.
No kernel may reach another device: no remote copies, remote signals or barrier semaphores. Data moves between devices by JAX's collectives and lax.ppermute only.
A program may use at most 32 MiB of HBM per device.

```python
import math
import jax
import jax.numpy as jnp
from jax import lax

CH = 4096
KW = 7
BANDS = 16
HID = 64
FEAT = 33
SEQ = 8192


def draw_filter_decay(key, part):
    subkeys = jax.random.split(key, 3)
    portion = 0.5
    chosen = jax.random.uniform(subkeys[0], (CH,)) < portion
    slower = jnp.exp(jax.random.uniform(subkeys[1], (CH,), minval=jnp.log(0.3 / SEQ), maxval=jnp.log(2.0 / SEQ)))
    faster = jnp.exp(jax.random.uniform(subkeys[2], (CH,), minval=jnp.log(1.0 / 50.0), maxval=jnp.log(1.0 / 30.0)))
    return jnp.where(chosen, slower, faster).astype(jnp.float32)


def block_scale(stream_key, dims, shards, low, top_value):
    def one(position, shards_of):
        steps = jax.random.uniform(jax.random.fold_in(jax.random.fold_in(stream_key, 6), position), (shards_of,), jnp.float32, low / len(shards), top_value / len(shards))
        return jnp.repeat(jnp.exp(steps), dims[position] // shards_of).reshape((-1,) + (1,) * (len(dims) - position - 1))

    level = one(*shards[0])
    for cut in shards[1:]:
        level = level * one(*cut)
    return level


def centred(key, extent, deviation, most, cuts=(), kind=jnp.bfloat16):
    level = block_scale(key, extent, cuts, -0.22, 0.18) if cuts else 1.0
    array = jax.random.normal(key, extent, jnp.float32) * deviation * level
    return jnp.minimum(jnp.maximum(array, -most), most).astype(kind)


def setup_inputs(seed: int = 0) -> dict:
    key_list = jax.random.split(jax.random.key(seed), 8)
    projected = centred(key_list[0], (SEQ, 3, CH), 1.0, 6.0, ((0, 64), (2, 16)))
    short_weight = centred(key_list[1], (KW, 3, CH), 0.4, 2.5, ((2, 16),), jnp.float32)
    filter_in = centred(key_list[2], (FEAT, HID), FEAT ** -0.5, 1.0, (), jnp.float32)
    filter_bias = jnp.clip(jax.random.uniform(key_list[3], (HID,), jnp.float32, -3.140625, 3.140625), -3.140625, 3.140625)
    filter_out = centred(key_list[4], (HID, CH), HID ** -0.5, 0.75, ((1, 16),), jnp.float32)
    filter_decay = draw_filter_decay(jax.random.fold_in(key_list[7], 71), 0)
    cotangent = centred(key_list[6], (SEQ, CH), 1.0, 6.0, ((0, 64), (1, 16)))
    return {"projected": projected, "short_weight": short_weight, "filter_in": filter_in, "filter_bias": filter_bias, "filter_out": filter_out, "filter_decay": filter_decay, "cotangent": cotangent}


full_turn = 6.283185307179586

def filter_features(places, bands):
    columns = [places.astype(jnp.float32) / SEQ]
    for band in range(bands):
        stride = min(2 ** band, SEQ // 4)
        phases = places % (SEQ // stride) * stride
        angles = full_turn / SEQ * phases.astype(jnp.float32)
        columns.append(jnp.cos(angles))
        columns.append(jnp.sin(angles))
    return jnp.stack(columns, axis=1)

def reference(projected, short_weight, filter_in, filter_bias, filter_out, filter_decay, cotangent):
    places = jnp.arange(SEQ, dtype=jnp.int32)
    features = filter_features(places, BANDS)
    activity = jnp.sin(jnp.dot(features, filter_in, precision=lax.Precision.HIGHEST) + filter_bias)
    shaped = jnp.dot(activity, filter_out, precision=lax.Precision.HIGHEST)
    window = jnp.exp(-filter_decay[None, :] * places.astype(jnp.float32)[:, None])
    window = window * jnp.sqrt(-jnp.expm1(-2.0 * filter_decay))[None, :]
    long_filter = shaped * window
    lead = KW - 1
    padded = jnp.concatenate([jnp.zeros((lead, 3, CH), jnp.bfloat16), projected], axis=0)
    mixed = jnp.zeros((SEQ, 3, CH), jnp.float32)
    for offset in range(KW):
        mixed = mixed + short_weight[offset] * padded[lead - offset:lead - offset + SEQ]
    query = mixed[:, 0]
    key_part = mixed[:, 1]
    value_part = mixed[:, 2]
    product = key_part * value_part
    padded_length = 2 * SEQ
    signal_spec = jnp.fft.rfft(product, n=padded_length, axis=0)
    filter_spec = jnp.fft.rfft(long_filter, n=padded_length, axis=0)
    conv = jnp.fft.irfft(signal_spec * filter_spec, n=padded_length, axis=0)[:SEQ]
    operator_out = (query * conv).astype(jnp.bfloat16)
    grad_conv = cotangent * query
    grad_query = cotangent * conv
    grad_spec = jnp.fft.rfft(grad_conv, n=padded_length, axis=0)
    grad_product = jnp.fft.irfft(jnp.conj(filter_spec) * grad_spec, n=padded_length, axis=0)[:SEQ]
    grad_filter = jnp.fft.irfft(grad_spec * jnp.conj(signal_spec), n=padded_length, axis=0)[:SEQ] / math.sqrt(SEQ)
    grad_mixed = jnp.stack([grad_query, grad_product * value_part, grad_product * key_part], axis=1)
    tailed = jnp.concatenate([grad_mixed, jnp.zeros((lead, 3, CH), grad_mixed.dtype)], axis=0)
    grad_projected = jnp.zeros((SEQ, 3, CH), jnp.float32)
    for offset in range(KW):
        grad_projected = grad_projected + short_weight[offset] * tailed[offset:offset + SEQ]
    return (operator_out, grad_projected.astype(jnp.bfloat16), grad_filter)
```

```python
import math

import jax
import jax.numpy as jnp
from jax import lax
from jax.sharding import PartitionSpec as P

exact_mode = lax.Precision.HIGHEST
full_turn = 6.283185307179586


def passed_along(value, axis, by):
    length = lax.axis_size(axis)
    pairs = [(i, i + by) for i in range(length) if 0 <= i + by < length]
    return lax.ppermute(value, axis, pairs)


def turning(numbers, period, direction):
    angles = direction * full_turn / period * (numbers % period).astype(jnp.float32)
    return (jnp.cos(angles), jnp.sin(angles))


def rotate(values, cosine, sine):
    return jnp.stack([values[0] * cosine - values[1] * sine, values[0] * sine + values[1] * cosine])


def times_complex(first, second):
    return jnp.stack(
        [first[0] * second[0] - first[1] * second[1], first[0] * second[1] + first[1] * second[0]]
    )


def conjugate(values):
    return jnp.stack([values[0], -values[1]])


def mix_axis(values, count, direction, pattern):
    index = jnp.arange(count, dtype=jnp.int32)
    cosine, sine = turning(index[:, None] * index[None, :], count, direction)
    real_part = jnp.einsum(pattern, cosine, values[0], precision=exact_mode) - jnp.einsum(
        pattern, sine, values[1], precision=exact_mode
    )
    other_part = jnp.einsum(pattern, cosine, values[1], precision=exact_mode) + jnp.einsum(
        pattern, sine, values[0], precision=exact_mode
    )
    return jnp.stack([real_part, other_part])


def grid_places(parts, length):
    return (
        jnp.arange(parts, dtype=jnp.int32)[:, None] * length
        + jnp.arange(length, dtype=jnp.int32)[None, :]
    )


def forward_padded(signal):
    parts = signal.shape[1]
    length = signal.shape[2]
    seq_total = parts * length
    cosine, sine = turning(grid_places(parts, length), 2 * seq_total, -1.0)
    values = jnp.stack(
        [jnp.stack([signal, signal * cosine]), jnp.stack([jnp.zeros_like(signal), signal * sine])]
    )
    values = mix_axis(values, parts, -1.0, "ap,hrpj->hraj")
    index_a = jnp.arange(parts, dtype=jnp.int32)[:, None]
    index_j = jnp.arange(length, dtype=jnp.int32)[None, :]
    cosine, sine = turning(index_a * index_j, seq_total, -1.0)
    values = rotate(values, cosine, sine)
    return mix_axis(values, length, -1.0, "bj,hraj->hrab")


def inverse_padded(spectrum):
    parts = spectrum.shape[3]
    length = spectrum.shape[4]
    seq_total = parts * length
    values = mix_axis(spectrum, length, 1.0, "jb,hrab->hraj")
    index_a = jnp.arange(parts, dtype=jnp.int32)[:, None]
    index_j = jnp.arange(length, dtype=jnp.int32)[None, :]
    cosine, sine = turning(index_a * index_j, seq_total, 1.0)
    values = rotate(values, cosine, sine)
    values = mix_axis(values, parts, 1.0, "pa,hraj->hrpj") / seq_total
    cosine, sine = turning(grid_places(parts, length), 2 * seq_total, 1.0)
    return 0.5 * (values[0, 0] + values[0, 1] * cosine - values[1, 1] * sine)


def to_channels(stacked):
    return lax.all_to_all(
        jnp.swapaxes(stacked, 1, 2)[:, :, None, :], "inner", split_axis=1, concat_axis=2, tiled=True
    )


def to_positions(values):
    moved = lax.all_to_all(values, "inner", split_axis=2, concat_axis=1, tiled=True)
    return jnp.swapaxes(moved[:, :, 0, :], 1, 2)


def filter_features(places, seq_total, bands):
    columns = [places.astype(jnp.float32) / seq_total]
    for band in range(bands):
        stride = min(2**band, seq_total // 4)
        phases = places % (seq_total // stride) * stride
        angles = full_turn / seq_total * phases.astype(jnp.float32)
        columns.append(jnp.cos(angles))
        columns.append(jnp.sin(angles))
    return jnp.stack(columns, axis=1)


def decay_window(rates, places):
    return jnp.exp(-rates * places.astype(jnp.float32)) * jnp.sqrt(-jnp.expm1(-2.0 * rates))


def body(projected, short_weight, filter_in, filter_bias, filter_out, filter_decay, cotangent):
    parts = lax.axis_size("inner")
    inner_id = lax.axis_index("inner")
    length = projected.shape[0]
    chans = projected.shape[2]
    taps = short_weight.shape[0]
    bands = (filter_in.shape[0] - 1) // 2
    seq_total = parts * length
    slices = chans // parts
    earlier = passed_along(projected[length - taps + 1 :], "inner", 1)
    extended = jnp.concatenate([earlier, projected], axis=0)
    mixed = jnp.zeros((length, 3, chans), jnp.float32)
    for offset in range(taps):
        mixed = (
            mixed + short_weight[offset] * extended[taps - 1 - offset : taps - 1 - offset + length]
        )
    query = mixed[:, 0]
    key_part = mixed[:, 1]
    value_part = mixed[:, 2]
    product = key_part * value_part
    grad_conv = cotangent * query
    moved = to_channels(jnp.stack([product, grad_conv]))
    signal_rows = moved[0]
    grad_rows = moved[1]
    first = inner_id * slices
    all_places = jnp.arange(seq_total, dtype=jnp.int32)
    features = jnp.transpose(filter_features(all_places, seq_total, bands))
    activity = jnp.sin(
        jnp.dot(jnp.transpose(filter_in), features, precision=exact_mode) + filter_bias[:, None]
    )
    own_out = lax.dynamic_slice_in_dim(filter_out, first, slices, axis=1)
    own_decay = lax.dynamic_slice_in_dim(filter_decay, first, slices)
    shaped = jnp.dot(jnp.transpose(own_out), activity, precision=exact_mode)
    long_filter = shaped * decay_window(own_decay[:, None], all_places[None, :])
    filter_rows = long_filter.reshape(slices, parts, length)
    spectra = forward_padded(jnp.concatenate([signal_rows, filter_rows, grad_rows], axis=0))
    signal_spec = spectra[:, :, :slices]
    filter_spec = spectra[:, :, slices : 2 * slices]
    grad_spec = spectra[:, :, 2 * slices :]
    paired = jnp.concatenate(
        [
            times_complex(signal_spec, filter_spec),
            times_complex(conjugate(filter_spec), grad_spec),
            times_complex(grad_spec, conjugate(signal_spec)),
        ],
        axis=2,
    )
    returned = inverse_padded(paired)
    back = to_positions(returned.reshape(3, slices, parts, length))
    conv = back[0]
    grad_product = back[1]
    grad_filter = back[2] / math.sqrt(seq_total)
    operator_out = (query * conv).astype(jnp.bfloat16)
    grad_query = cotangent * conv
    grad_mixed = jnp.stack([grad_query, grad_product * value_part, grad_product * key_part], axis=1)
    later = passed_along(grad_mixed[: taps - 1], "inner", -1)
    tailed = jnp.concatenate([grad_mixed, later], axis=0)
    grad_projected = jnp.zeros((length, 3, chans), jnp.float32)
    for offset in range(taps):
        grad_projected = grad_projected + short_weight[offset] * tailed[offset : offset + length]
    return (operator_out, grad_projected.astype(jnp.bfloat16), grad_filter)


def solution(mesh):
    in_specs = (
        P("inner", None, "outer"),
        P(None, None, "outer"),
        P(),
        P(),
        P(None, "outer"),
        P("outer"),
        P("inner", "outer"),
    )
    out_specs = (P("inner", "outer"), P("inner", None, "outer"), P("inner", "outer"))
    return jax.shard_map(body, mesh=mesh, in_specs=in_specs, out_specs=out_specs, check_vma=False)
```

```python
import math

import jax
import jax.numpy as jnp
from jax import lax
from jax.sharding import PartitionSpec as P

exact_mode = lax.Precision.HIGHEST
full_turn = 6.283185307179586


def passed_along(value, axis, by):
    length = lax.axis_size(axis)
    pairs = [(i, i + by) for i in range(length) if 0 <= i + by < length]
    return lax.ppermute(value, axis, pairs)


def turning(numbers, period, direction):
    angles = direction * full_turn / period * (numbers % period).astype(jnp.float32)
    return (jnp.cos(angles), jnp.sin(angles))


def rotate(values, cosine, sine):
    return jnp.stack([values[0] * cosine - values[1] * sine, values[0] * sine + values[1] * cosine])


def times_complex(first, second):
    return jnp.stack(
        [first[0] * second[0] - first[1] * second[1], first[0] * second[1] + first[1] * second[0]]
    )


def conjugate(values):
    return jnp.stack([values[0], -values[1]])


def mix_axis(values, count, direction, pattern):
    index = jnp.arange(count, dtype=jnp.int32)
    cosine, sine = turning(index[:, None] * index[None, :], count, direction)
    real_part = jnp.einsum(pattern, cosine, values[0], precision=exact_mode) - jnp.einsum(
        pattern, sine, values[1], precision=exact_mode
    )
    other_part = jnp.einsum(pattern, cosine, values[1], precision=exact_mode) + jnp.einsum(
        pattern, sine, values[0], precision=exact_mode
    )
    return jnp.stack([real_part, other_part])


def grid_places(parts, length):
    return (
        jnp.arange(parts, dtype=jnp.int32)[:, None] * length
        + jnp.arange(length, dtype=jnp.int32)[None, :]
    )


def forward_padded(signal):
    parts = signal.shape[1]
    length = signal.shape[2]
    seq_total = parts * length
    cosine, sine = turning(grid_places(parts, length), 2 * seq_total, -1.0)
    values = jnp.stack(
        [jnp.stack([signal, signal * cosine]), jnp.stack([jnp.zeros_like(signal), signal * sine])]
    )
    values = mix_axis(values, parts, -1.0, "ap,hrpj->hraj")
    index_a = jnp.arange(parts, dtype=jnp.int32)[:, None]
    index_j = jnp.arange(length, dtype=jnp.int32)[None, :]
    cosine, sine = turning(index_a * index_j, seq_total, -1.0)
    values = rotate(values, cosine, sine)
    return mix_axis(values, length, -1.0, "bj,hraj->hrab")


def inverse_padded(spectrum):
    parts = spectrum.shape[3]
    length = spectrum.shape[4]
    seq_total = parts * length
    values = mix_axis(spectrum, length, 1.0, "jb,hrab->hraj")
    index_a = jnp.arange(parts, dtype=jnp.int32)[:, None]
    index_j = jnp.arange(length, dtype=jnp.int32)[None, :]
    cosine, sine = turning(index_a * index_j, seq_total, 1.0)
    values = rotate(values, cosine, sine)
    values = mix_axis(values, parts, 1.0, "pa,hraj->hrpj") / seq_total
    cosine, sine = turning(grid_places(parts, length), 2 * seq_total, 1.0)
    return 0.5 * (values[0, 0] + values[0, 1] * cosine - values[1, 1] * sine)


def to_channels(stacked):
    return lax.all_to_all(
        jnp.swapaxes(stacked, 1, 2)[:, :, None, :], "inner", split_axis=1, concat_axis=2, tiled=True
    )


def to_positions(values):
    moved = lax.all_to_all(values, "inner", split_axis=2, concat_axis=1, tiled=True)
    return jnp.swapaxes(moved[:, :, 0, :], 1, 2)


def filter_features(places, seq_total, bands):
    columns = [places.astype(jnp.float32) / seq_total]
    for band in range(bands):
        stride = min(2**band, seq_total // 4)
        phases = places % (seq_total // stride) * stride
        angles = full_turn / seq_total * phases.astype(jnp.float32)
        columns.append(jnp.cos(angles))
        columns.append(jnp.sin(angles))
    return jnp.stack(columns, axis=1)


def decay_window(rates, places):
    return jnp.exp(-rates * places.astype(jnp.float32)) * jnp.sqrt(-jnp.expm1(-2.0 * rates))


def body(projected, short_weight, filter_in, filter_bias, filter_out, filter_decay, cotangent):
    parts = lax.axis_size("inner")
    inner_id = lax.axis_index("inner")
    length = projected.shape[0]
    chans = projected.shape[2]
    taps = short_weight.shape[0]
    bands = (filter_in.shape[0] - 1) // 2
    seq_total = parts * length
    slices = chans // parts
    earlier = passed_along(projected[length - taps + 1 :], "inner", 1)
    extended = jnp.concatenate([earlier, projected], axis=0)
    mixed = jnp.zeros((length, 3, chans), jnp.float32)
    for offset in range(taps):
        mixed = (
            mixed + short_weight[offset] * extended[taps - 1 - offset : taps - 1 - offset + length]
        )
    query = mixed[:, 0]
    key_part = mixed[:, 1]
    value_part = mixed[:, 2]
    product = key_part * value_part
    grad_conv = cotangent * query
    places = inner_id * length + jnp.arange(length, dtype=jnp.int32)
    activity = jnp.sin(
        jnp.dot(filter_features(places, seq_total, bands), filter_in, precision=exact_mode)
        + filter_bias
    )
    shaped = jnp.dot(activity, filter_out, precision=exact_mode)
    long_filter = shaped * decay_window(filter_decay[None, :], places[:, None])
    moved = to_channels(jnp.stack([product, long_filter, grad_conv]))
    signal_rows = moved[0]
    filter_rows = moved[1]
    grad_rows = moved[2]
    spectra = forward_padded(jnp.concatenate([signal_rows, filter_rows, grad_rows], axis=0))
    signal_spec = spectra[:, :, :slices]
    filter_spec = spectra[:, :, slices : 2 * slices]
    grad_spec = spectra[:, :, 2 * slices :]
    paired = jnp.concatenate(
        [
            times_complex(signal_spec, filter_spec),
            times_complex(conjugate(filter_spec), grad_spec),
            times_complex(grad_spec, conjugate(signal_spec)),
        ],
        axis=2,
    )
    returned = inverse_padded(paired)
    back = to_positions(returned.reshape(3, slices, parts, length))
    conv = back[0]
    grad_product = back[1]
    grad_filter = back[2] / math.sqrt(seq_total)
    operator_out = (query * conv).astype(jnp.bfloat16)
    grad_query = cotangent * conv
    grad_mixed = jnp.stack([grad_query, grad_product * value_part, grad_product * key_part], axis=1)
    later = passed_along(grad_mixed[: taps - 1], "inner", -1)
    tailed = jnp.concatenate([grad_mixed, later], axis=0)
    grad_projected = jnp.zeros((length, 3, chans), jnp.float32)
    for offset in range(taps):
        grad_projected = grad_projected + short_weight[offset] * tailed[offset : offset + length]
    return (operator_out, grad_projected.astype(jnp.bfloat16), grad_filter)


def solution(mesh):
    in_specs = (
        P("inner", None, "outer"),
        P(None, None, "outer"),
        P(),
        P(),
        P(None, "outer"),
        P("outer"),
        P("inner", "outer"),
    )
    out_specs = (P("inner", "outer"), P("inner", None, "outer"), P("inner", "outer"))
    return jax.shard_map(body, mesh=mesh, in_specs=in_specs, out_specs=out_specs, check_vma=False)
```

```python
import math

import jax
import jax.numpy as jnp
from jax import lax
from jax.sharding import PartitionSpec as P

exact_mode = lax.Precision.HIGHEST
transform_mode = lax.Precision.HIGH
full_turn = 6.283185307179586


def passed_along(value, axis, by):
    length = lax.axis_size(axis)
    pairs = [(i, i + by) for i in range(length) if 0 <= i + by < length]
    return lax.ppermute(value, axis, pairs)


def turning(numbers, period, direction):
    angles = direction * full_turn / period * (numbers % period).astype(jnp.float32)
    return (jnp.cos(angles), jnp.sin(angles))


def rotate(values, cosine, sine):
    return jnp.stack([values[0] * cosine - values[1] * sine, values[0] * sine + values[1] * cosine])


def times_complex(first, second):
    return jnp.stack(
        [first[0] * second[0] - first[1] * second[1], first[0] * second[1] + first[1] * second[0]]
    )


def conjugate(values):
    return jnp.stack([values[0], -values[1]])


def mix_axis(values, count, direction, pattern):
    index = jnp.arange(count, dtype=jnp.int32)
    cosine, sine = turning(index[:, None] * index[None, :], count, direction)
    real_part = jnp.einsum(pattern, cosine, values[0], precision=transform_mode) - jnp.einsum(
        pattern, sine, values[1], precision=transform_mode
    )
    other_part = jnp.einsum(pattern, cosine, values[1], precision=transform_mode) + jnp.einsum(
        pattern, sine, values[0], precision=transform_mode
    )
    return jnp.stack([real_part, other_part])


def grid_places(parts, length):
    return (
        jnp.arange(parts, dtype=jnp.int32)[:, None] * length
        + jnp.arange(length, dtype=jnp.int32)[None, :]
    )


def forward_padded(signal):
    parts = signal.shape[1]
    length = signal.shape[2]
    seq_total = parts * length
    cosine, sine = turning(grid_places(parts, length), 2 * seq_total, -1.0)
    values = jnp.stack(
        [jnp.stack([signal, signal * cosine]), jnp.stack([jnp.zeros_like(signal), signal * sine])]
    )
    values = mix_axis(values, parts, -1.0, "ap,hrpj->hraj")
    index_a = jnp.arange(parts, dtype=jnp.int32)[:, None]
    index_j = jnp.arange(length, dtype=jnp.int32)[None, :]
    cosine, sine = turning(index_a * index_j, seq_total, -1.0)
    values = rotate(values, cosine, sine)
    return mix_axis(values, length, -1.0, "bj,hraj->hrab")


def inverse_padded(spectrum):
    parts = spectrum.shape[3]
    length = spectrum.shape[4]
    seq_total = parts * length
    values = mix_axis(spectrum, length, 1.0, "jb,hrab->hraj")
    index_a = jnp.arange(parts, dtype=jnp.int32)[:, None]
    index_j = jnp.arange(length, dtype=jnp.int32)[None, :]
    cosine, sine = turning(index_a * index_j, seq_total, 1.0)
    values = rotate(values, cosine, sine)
    values = mix_axis(values, parts, 1.0, "pa,hraj->hrpj") / seq_total
    cosine, sine = turning(grid_places(parts, length), 2 * seq_total, 1.0)
    return 0.5 * (values[0, 0] + values[0, 1] * cosine - values[1, 1] * sine)


def to_channels(stacked):
    return lax.all_to_all(
        jnp.swapaxes(stacked, 1, 2)[:, :, None, :], "inner", split_axis=1, concat_axis=2, tiled=True
    )


def to_positions(values):
    moved = lax.all_to_all(values, "inner", split_axis=2, concat_axis=1, tiled=True)
    return jnp.swapaxes(moved[:, :, 0, :], 1, 2)


def filter_features(places, seq_total, bands):
    columns = [places.astype(jnp.float32) / seq_total]
    for band in range(bands):
        stride = min(2**band, seq_total // 4)
        phases = places % (seq_total // stride) * stride
        angles = full_turn / seq_total * phases.astype(jnp.float32)
        columns.append(jnp.cos(angles))
        columns.append(jnp.sin(angles))
    return jnp.stack(columns, axis=1)


def decay_window(rates, places):
    return jnp.exp(-rates * places.astype(jnp.float32)) * jnp.sqrt(-jnp.expm1(-2.0 * rates))


def body(projected, short_weight, filter_in, filter_bias, filter_out, filter_decay, cotangent):
    parts = lax.axis_size("inner")
    inner_id = lax.axis_index("inner")
    length = projected.shape[0]
    chans = projected.shape[2]
    taps = short_weight.shape[0]
    bands = (filter_in.shape[0] - 1) // 2
    seq_total = parts * length
    slices = chans // parts
    earlier = passed_along(projected[length - taps + 1 :], "inner", 1)
    extended = jnp.concatenate([earlier, projected], axis=0)
    mixed = jnp.zeros((length, 3, chans), jnp.float32)
    for offset in range(taps):
        mixed = (
            mixed + short_weight[offset] * extended[taps - 1 - offset : taps - 1 - offset + length]
        )
    query = mixed[:, 0]
    key_part = mixed[:, 1]
    value_part = mixed[:, 2]
    product = key_part * value_part
    grad_conv = cotangent * query
    places = inner_id * length + jnp.arange(length, dtype=jnp.int32)
    activity = jnp.sin(
        jnp.dot(filter_features(places, seq_total, bands), filter_in, precision=exact_mode)
        + filter_bias
    )
    shaped = jnp.dot(activity, filter_out, precision=exact_mode)
    long_filter = shaped * decay_window(filter_decay[None, :], places[:, None])
    moved = to_channels(jnp.stack([product, long_filter, grad_conv]))
    signal_rows = moved[0]
    filter_rows = moved[1]
    grad_rows = moved[2]
    spectra = forward_padded(jnp.concatenate([signal_rows, filter_rows, grad_rows], axis=0))
    signal_spec = spectra[:, :, :slices]
    filter_spec = spectra[:, :, slices : 2 * slices]
    grad_spec = spectra[:, :, 2 * slices :]
    paired = jnp.concatenate(
        [
            times_complex(signal_spec, filter_spec),
            times_complex(conjugate(filter_spec), grad_spec),
            times_complex(grad_spec, conjugate(signal_spec)),
        ],
        axis=2,
    )
    returned = inverse_padded(paired)
    back = to_positions(returned.reshape(3, slices, parts, length))
    conv = back[0]
    grad_product = back[1]
    grad_filter = back[2] / math.sqrt(seq_total)
    operator_out = (query * conv).astype(jnp.bfloat16)
    grad_query = cotangent * conv
    grad_mixed = jnp.stack([grad_query, grad_product * value_part, grad_product * key_part], axis=1)
    later = passed_along(grad_mixed[: taps - 1], "inner", -1)
    tailed = jnp.concatenate([grad_mixed, later], axis=0)
    grad_projected = jnp.zeros((length, 3, chans), jnp.float32)
    for offset in range(taps):
        grad_projected = grad_projected + short_weight[offset] * tailed[offset : offset + length]
    return (operator_out, grad_projected.astype(jnp.bfloat16), grad_filter)


def solution(mesh):
    in_specs = (
        P("inner", None, "outer"),
        P(None, None, "outer"),
        P(),
        P(),
        P(None, "outer"),
        P("outer"),
        P("inner", "outer"),
    )
    out_specs = (P("inner", "outer"), P("inner", None, "outer"), P("inner", "outer"))
    return jax.shard_map(body, mesh=mesh, in_specs=in_specs, out_specs=out_specs, check_vma=False)
```

```python
import math

import jax
import jax.numpy as jnp
from jax import lax
from jax.sharding import PartitionSpec as P

exact_mode = lax.Precision.HIGHEST
transform_mode = lax.Precision.HIGH
full_turn = 6.283185307179586


def passed_along(value, axis, by):
    length = lax.axis_size(axis)
    pairs = [(i, i + by) for i in range(length) if 0 <= i + by < length]
    return lax.ppermute(value, axis, pairs)


def turning(numbers, period, direction):
    angles = direction * full_turn / period * (numbers % period).astype(jnp.float32)
    return (jnp.cos(angles), jnp.sin(angles))


def rotate(values, cosine, sine):
    return jnp.stack([values[0] * cosine - values[1] * sine, values[0] * sine + values[1] * cosine])


def times_complex(first, second):
    return jnp.stack(
        [first[0] * second[0] - first[1] * second[1], first[0] * second[1] + first[1] * second[0]]
    )


def conjugate(values):
    return jnp.stack([values[0], -values[1]])


def mix_axis(values, count, direction, pattern):
    index = jnp.arange(count, dtype=jnp.int32)
    cosine, sine = turning(index[:, None] * index[None, :], count, direction)
    real_part = jnp.einsum(pattern, cosine, values[0], precision=transform_mode) - jnp.einsum(
        pattern, sine, values[1], precision=transform_mode
    )
    other_part = jnp.einsum(pattern, cosine, values[1], precision=transform_mode) + jnp.einsum(
        pattern, sine, values[0], precision=transform_mode
    )
    return jnp.stack([real_part, other_part])


def grid_places(parts, length):
    return (
        jnp.arange(parts, dtype=jnp.int32)[:, None] * length
        + jnp.arange(length, dtype=jnp.int32)[None, :]
    )


def forward_padded(signal):
    parts = signal.shape[1]
    length = signal.shape[2]
    seq_total = parts * length
    cosine, sine = turning(grid_places(parts, length), 2 * seq_total, -1.0)
    values = jnp.stack(
        [jnp.stack([signal, signal * cosine]), jnp.stack([jnp.zeros_like(signal), signal * sine])]
    )
    values = mix_axis(values, parts, -1.0, "ap,hrpj->hraj")
    index_a = jnp.arange(parts, dtype=jnp.int32)[:, None]
    index_j = jnp.arange(length, dtype=jnp.int32)[None, :]
    cosine, sine = turning(index_a * index_j, seq_total, -1.0)
    values = rotate(values, cosine, sine)
    return mix_axis(values, length, -1.0, "bj,hraj->hrab")


def inverse_padded(spectrum):
    half = spectrum.shape[2] // 2
    first = spectrum[:, :, :half]
    second = spectrum[:, :, half:]
    joined = jnp.stack([first[0] - second[1], first[1] + second[0]])
    parts = spectrum.shape[3]
    length = spectrum.shape[4]
    seq_total = parts * length
    values = mix_axis(joined, length, 1.0, "jb,hrab->hraj")
    index_a = jnp.arange(parts, dtype=jnp.int32)[:, None]
    index_j = jnp.arange(length, dtype=jnp.int32)[None, :]
    cosine, sine = turning(index_a * index_j, seq_total, 1.0)
    values = rotate(values, cosine, sine)
    values = mix_axis(values, parts, 1.0, "pa,hraj->hrpj") / seq_total
    cosine, sine = turning(grid_places(parts, length), 2 * seq_total, 1.0)
    real_part = 0.5 * (values[0, 0] + values[0, 1] * cosine - values[1, 1] * sine)
    other_part = 0.5 * (values[1, 0] + values[0, 1] * sine + values[1, 1] * cosine)
    return jnp.concatenate([real_part, other_part], axis=0)


def to_channels(stacked):
    return lax.all_to_all(
        jnp.swapaxes(stacked, 1, 2)[:, :, None, :], "inner", split_axis=1, concat_axis=2, tiled=True
    )


def to_positions(values):
    moved = lax.all_to_all(values, "inner", split_axis=2, concat_axis=1, tiled=True)
    return jnp.swapaxes(moved[:, :, 0, :], 1, 2)


def filter_features(places, seq_total, bands):
    columns = [places.astype(jnp.float32) / seq_total]
    for band in range(bands):
        stride = min(2**band, seq_total // 4)
        phases = places % (seq_total // stride) * stride
        angles = full_turn / seq_total * phases.astype(jnp.float32)
        columns.append(jnp.cos(angles))
        columns.append(jnp.sin(angles))
    return jnp.stack(columns, axis=1)


def decay_window(rates, places):
    return jnp.exp(-rates * places.astype(jnp.float32)) * jnp.sqrt(-jnp.expm1(-2.0 * rates))


def body(projected, short_weight, filter_in, filter_bias, filter_out, filter_decay, cotangent):
    parts = lax.axis_size("inner")
    inner_id = lax.axis_index("inner")
    length = projected.shape[0]
    chans = projected.shape[2]
    taps = short_weight.shape[0]
    bands = (filter_in.shape[0] - 1) // 2
    seq_total = parts * length
    slices = chans // parts
    earlier = passed_along(projected[length - taps + 1 :], "inner", 1)
    extended = jnp.concatenate([earlier, projected], axis=0)
    mixed = jnp.zeros((length, 3, chans), jnp.float32)
    for offset in range(taps):
        mixed = (
            mixed + short_weight[offset] * extended[taps - 1 - offset : taps - 1 - offset + length]
        )
    query = mixed[:, 0]
    key_part = mixed[:, 1]
    value_part = mixed[:, 2]
    product = key_part * value_part
    grad_conv = cotangent * query
    places = inner_id * length + jnp.arange(length, dtype=jnp.int32)
    activity = jnp.sin(
        jnp.dot(filter_features(places, seq_total, bands), filter_in, precision=exact_mode)
        + filter_bias
    )
    shaped = jnp.dot(activity, filter_out, precision=exact_mode)
    long_filter = shaped * decay_window(filter_decay[None, :], places[:, None])
    moved = to_channels(jnp.stack([product, long_filter, grad_conv]))
    signal_rows = moved[0]
    filter_rows = moved[1]
    grad_rows = moved[2]
    spectra = forward_padded(jnp.concatenate([signal_rows, filter_rows, grad_rows], axis=0))
    signal_spec = spectra[:, :, :slices]
    filter_spec = spectra[:, :, slices : 2 * slices]
    grad_spec = spectra[:, :, 2 * slices :]
    paired = jnp.concatenate(
        [
            times_complex(signal_spec, filter_spec),
            times_complex(conjugate(filter_spec), grad_spec),
            times_complex(grad_spec, conjugate(signal_spec)),
        ],
        axis=2,
    )
    spread = slices // 2
    ordered = jnp.concatenate(
        [paired[:, :, : slices], paired[:, :, 2 * slices : 2 * slices + spread],
         paired[:, :, slices : 2 * slices], paired[:, :, 2 * slices + spread :]],
        axis=2,
    )
    returned = inverse_padded(ordered)
    returned = jnp.concatenate(
        [returned[:slices], returned[slices + spread : 2 * slices + spread],
         returned[slices : slices + spread], returned[2 * slices + spread :]],
        axis=0,
    )
    back = to_positions(returned.reshape(3, slices, parts, length))
    conv = back[0]
    grad_product = back[1]
    grad_filter = back[2] / math.sqrt(seq_total)
    operator_out = (query * conv).astype(jnp.bfloat16)
    grad_query = cotangent * conv
    grad_mixed = jnp.stack([grad_query, grad_product * value_part, grad_product * key_part], axis=1)
    later = passed_along(grad_mixed[: taps - 1], "inner", -1)
    tailed = jnp.concatenate([grad_mixed, later], axis=0)
    grad_projected = jnp.zeros((length, 3, chans), jnp.float32)
    for offset in range(taps):
        grad_projected = grad_projected + short_weight[offset] * tailed[offset : offset + length]
    return (operator_out, grad_projected.astype(jnp.bfloat16), grad_filter)


def solution(mesh):
    in_specs = (
        P("inner", None, "outer"),
        P(None, None, "outer"),
        P(),
        P(),
        P(None, "outer"),
        P("outer"),
        P("inner", "outer"),
    )
    out_specs = (P("inner", "outer"), P("inner", None, "outer"), P("inner", "outer"))
    return jax.shard_map(body, mesh=mesh, in_specs=in_specs, out_specs=out_specs, check_vma=False)
```

```python
import math

import jax
import jax.numpy as jnp
from jax import lax
from jax.sharding import PartitionSpec as P

exact_mode = lax.Precision.HIGHEST
transform_mode = lax.Precision.HIGH
full_turn = 6.283185307179586


def passed_along(value, axis, by):
    length = lax.axis_size(axis)
    pairs = [(i, i + by) for i in range(length) if 0 <= i + by < length]
    return lax.ppermute(value, axis, pairs)


def turning(numbers, period, direction):
    angles = direction * full_turn / period * (numbers % period).astype(jnp.float32)
    return (jnp.cos(angles), jnp.sin(angles))


def rotate(values, cosine, sine):
    return jnp.stack([values[0] * cosine - values[1] * sine, values[0] * sine + values[1] * cosine])


def times_complex(first, second):
    return jnp.stack(
        [first[0] * second[0] - first[1] * second[1], first[0] * second[1] + first[1] * second[0]]
    )


def conjugate(values):
    return jnp.stack([values[0], -values[1]])


def mix_axis(values, count, direction, pattern):
    index = jnp.arange(count, dtype=jnp.int32)
    cosine, sine = turning(index[:, None] * index[None, :], count, direction)
    real_part = jnp.einsum(pattern, cosine, values[0], precision=transform_mode) - jnp.einsum(
        pattern, sine, values[1], precision=transform_mode
    )
    other_part = jnp.einsum(pattern, cosine, values[1], precision=transform_mode) + jnp.einsum(
        pattern, sine, values[0], precision=transform_mode
    )
    return jnp.stack([real_part, other_part])


def grid_places(parts, length):
    return (
        jnp.arange(parts, dtype=jnp.int32)[:, None] * length
        + jnp.arange(length, dtype=jnp.int32)[None, :]
    )


def forward_padded(first, second):
    parts = first.shape[1]
    length = first.shape[2]
    seq_total = parts * length
    cosine, sine = turning(grid_places(parts, length), 2 * seq_total, -1.0)
    values = jnp.stack(
        [
            jnp.stack([first, first * cosine - second * sine]),
            jnp.stack([second, first * sine + second * cosine]),
        ]
    )
    values = mix_axis(values, parts, -1.0, "ap,hrpj->hraj")
    index_a = jnp.arange(parts, dtype=jnp.int32)[:, None]
    index_j = jnp.arange(length, dtype=jnp.int32)[None, :]
    cosine, sine = turning(index_a * index_j, seq_total, -1.0)
    values = rotate(values, cosine, sine)
    spectrum = mix_axis(values, length, -1.0, "bj,hraj->hrab")
    flipped = jnp.flip(spectrum[:, 0], axis=3)
    even_back = jnp.concatenate(
        [jnp.roll(flipped[:, :, :1], 1, axis=3), jnp.flip(flipped[:, :, 1:], axis=2)], axis=2
    )
    odd_back = jnp.flip(spectrum[:, 1], axis=(2, 3))
    mirrored = jnp.stack([even_back, odd_back], axis=1)
    first_spec = 0.5 * jnp.stack([spectrum[0] + mirrored[0], spectrum[1] - mirrored[1]])
    second_spec = 0.5 * jnp.stack([spectrum[1] + mirrored[1], mirrored[0] - spectrum[0]])
    return first_spec, second_spec


def inverse_padded(spectrum):
    half = spectrum.shape[2] // 2
    first = spectrum[:, :, :half]
    second = spectrum[:, :, half:]
    joined = jnp.stack([first[0] - second[1], first[1] + second[0]])
    parts = spectrum.shape[3]
    length = spectrum.shape[4]
    seq_total = parts * length
    values = mix_axis(joined, length, 1.0, "jb,hrab->hraj")
    index_a = jnp.arange(parts, dtype=jnp.int32)[:, None]
    index_j = jnp.arange(length, dtype=jnp.int32)[None, :]
    cosine, sine = turning(index_a * index_j, seq_total, 1.0)
    values = rotate(values, cosine, sine)
    values = mix_axis(values, parts, 1.0, "pa,hraj->hrpj") / seq_total
    cosine, sine = turning(grid_places(parts, length), 2 * seq_total, 1.0)
    real_part = 0.5 * (values[0, 0] + values[0, 1] * cosine - values[1, 1] * sine)
    other_part = 0.5 * (values[1, 0] + values[0, 1] * sine + values[1, 1] * cosine)
    return jnp.concatenate([real_part, other_part], axis=0)


def to_channels(stacked):
    return lax.all_to_all(
        jnp.swapaxes(stacked, 1, 2)[:, :, None, :], "inner", split_axis=1, concat_axis=2, tiled=True
    )


def to_positions(values):
    moved = lax.all_to_all(values, "inner", split_axis=2, concat_axis=1, tiled=True)
    return jnp.swapaxes(moved[:, :, 0, :], 1, 2)


def filter_features(places, seq_total, bands):
    columns = [places.astype(jnp.float32) / seq_total]
    for band in range(bands):
        stride = min(2**band, seq_total // 4)
        phases = places % (seq_total // stride) * stride
        angles = full_turn / seq_total * phases.astype(jnp.float32)
        columns.append(jnp.cos(angles))
        columns.append(jnp.sin(angles))
    return jnp.stack(columns, axis=1)


def decay_window(rates, places):
    return jnp.exp(-rates * places.astype(jnp.float32)) * jnp.sqrt(-jnp.expm1(-2.0 * rates))


def body(projected, short_weight, filter_in, filter_bias, filter_out, filter_decay, cotangent):
    parts = lax.axis_size("inner")
    inner_id = lax.axis_index("inner")
    length = projected.shape[0]
    chans = projected.shape[2]
    taps = short_weight.shape[0]
    bands = (filter_in.shape[0] - 1) // 2
    seq_total = parts * length
    slices = chans // parts
    earlier = passed_along(projected[length - taps + 1 :], "inner", 1)
    extended = jnp.concatenate([earlier, projected], axis=0)
    mixed = jnp.zeros((length, 3, chans), jnp.float32)
    for offset in range(taps):
        mixed = (
            mixed + short_weight[offset] * extended[taps - 1 - offset : taps - 1 - offset + length]
        )
    query = mixed[:, 0]
    key_part = mixed[:, 1]
    value_part = mixed[:, 2]
    product = key_part * value_part
    grad_conv = cotangent * query
    places = inner_id * length + jnp.arange(length, dtype=jnp.int32)
    activity = jnp.sin(
        jnp.dot(filter_features(places, seq_total, bands), filter_in, precision=exact_mode)
        + filter_bias
    )
    shaped = jnp.dot(activity, filter_out, precision=exact_mode)
    long_filter = shaped * decay_window(filter_decay[None, :], places[:, None])
    moved = to_channels(jnp.stack([product, long_filter, grad_conv]))
    signal_rows = moved[0]
    filter_rows = moved[1]
    grad_rows = moved[2]
    spread = slices // 2
    first_spec, second_spec = forward_padded(
        jnp.concatenate([signal_rows, filter_rows[:spread]], axis=0),
        jnp.concatenate([grad_rows, filter_rows[spread:]], axis=0),
    )
    signal_spec = first_spec[:, :, :slices]
    filter_spec = jnp.concatenate([first_spec[:, :, slices:], second_spec[:, :, slices:]], axis=2)
    grad_spec = second_spec[:, :, :slices]
    paired = jnp.concatenate(
        [
            times_complex(signal_spec, filter_spec),
            times_complex(conjugate(filter_spec), grad_spec),
            times_complex(grad_spec, conjugate(signal_spec)),
        ],
        axis=2,
    )
    ordered = jnp.concatenate(
        [paired[:, :, : slices], paired[:, :, 2 * slices : 2 * slices + spread],
         paired[:, :, slices : 2 * slices], paired[:, :, 2 * slices + spread :]],
        axis=2,
    )
    returned = inverse_padded(ordered)
    returned = jnp.concatenate(
        [returned[:slices], returned[slices + spread : 2 * slices + spread],
         returned[slices : slices + spread], returned[2 * slices + spread :]],
        axis=0,
    )
    back = to_positions(returned.reshape(3, slices, parts, length))
    conv = back[0]
    grad_product = back[1]
    grad_filter = back[2] / math.sqrt(seq_total)
    operator_out = (query * conv).astype(jnp.bfloat16)
    grad_query = cotangent * conv
    grad_mixed = jnp.stack([grad_query, grad_product * value_part, grad_product * key_part], axis=1)
    later = passed_along(grad_mixed[: taps - 1], "inner", -1)
    tailed = jnp.concatenate([grad_mixed, later], axis=0)
    grad_projected = jnp.zeros((length, 3, chans), jnp.float32)
    for offset in range(taps):
        grad_projected = grad_projected + short_weight[offset] * tailed[offset : offset + length]
    return (operator_out, grad_projected.astype(jnp.bfloat16), grad_filter)


def solution(mesh):
    in_specs = (
        P("inner", None, "outer"),
        P(None, None, "outer"),
        P(),
        P(),
        P(None, "outer"),
        P("outer"),
        P("inner", "outer"),
    )
    out_specs = (P("inner", "outer"), P("inner", None, "outer"), P("inner", "outer"))
    return jax.shard_map(body, mesh=mesh, in_specs=in_specs, out_specs=out_specs, check_vma=False)
```

```python
import math

import jax
import jax.numpy as jnp
from jax import lax
from jax.sharding import PartitionSpec as P

exact_mode = lax.Precision.HIGHEST
transform_mode = lax.Precision.HIGH
full_turn = 6.283185307179586


def passed_along(value, axis, by):
    length = lax.axis_size(axis)
    pairs = [(i, i + by) for i in range(length) if 0 <= i + by < length]
    return lax.ppermute(value, axis, pairs)


def turning(numbers, period, direction):
    angles = direction * full_turn / period * (numbers % period).astype(jnp.float32)
    return (jnp.cos(angles), jnp.sin(angles))


def rotate(values, cosine, sine):
    return jnp.stack([values[0] * cosine - values[1] * sine, values[0] * sine + values[1] * cosine])


def times_complex(first, second):
    return jnp.stack(
        [first[0] * second[0] - first[1] * second[1], first[0] * second[1] + first[1] * second[0]]
    )


def conjugate(values):
    return jnp.stack([values[0], -values[1]])


def mix_axis(values, count, direction, pattern):
    index = jnp.arange(count, dtype=jnp.int32)
    cosine, sine = turning(index[:, None] * index[None, :], count, direction)
    matrix = jnp.stack([jnp.stack([cosine, -sine]), jnp.stack([sine, cosine])])
    pair, result = pattern.split("->")
    table, operand = pair.split(",")
    joined = "zy" + table + ",y" + operand + "->z" + result
    return jnp.einsum(joined, matrix, values, precision=transform_mode)


def grid_places(parts, length):
    return (
        jnp.arange(parts, dtype=jnp.int32)[:, None] * length
        + jnp.arange(length, dtype=jnp.int32)[None, :]
    )


def forward_padded(signal):
    parts = signal.shape[1]
    length = signal.shape[2]
    seq_total = parts * length
    cosine, sine = turning(grid_places(parts, length), 2 * seq_total, -1.0)
    values = jnp.stack(
        [jnp.stack([signal, signal * cosine]), jnp.stack([jnp.zeros_like(signal), signal * sine])]
    )
    values = mix_axis(values, parts, -1.0, "ap,hrpj->hraj")
    index_a = jnp.arange(parts, dtype=jnp.int32)[:, None]
    index_j = jnp.arange(length, dtype=jnp.int32)[None, :]
    cosine, sine = turning(index_a * index_j, seq_total, -1.0)
    values = rotate(values, cosine, sine)
    return mix_axis(values, length, -1.0, "bj,hraj->hrab")


def inverse_padded(spectrum):
    half = spectrum.shape[2] // 2
    first = spectrum[:, :, :half]
    second = spectrum[:, :, half:]
    joined = jnp.stack([first[0] - second[1], first[1] + second[0]])
    parts = spectrum.shape[3]
    length = spectrum.shape[4]
    seq_total = parts * length
    values = mix_axis(joined, length, 1.0, "jb,hrab->hraj")
    index_a = jnp.arange(parts, dtype=jnp.int32)[:, None]
    index_j = jnp.arange(length, dtype=jnp.int32)[None, :]
    cosine, sine = turning(index_a * index_j, seq_total, 1.0)
    values = rotate(values, cosine, sine)
    values = mix_axis(values, parts, 1.0, "pa,hraj->hrpj") / seq_total
    cosine, sine = turning(grid_places(parts, length), 2 * seq_total, 1.0)
    real_part = 0.5 * (values[0, 0] + values[0, 1] * cosine - values[1, 1] * sine)
    other_part = 0.5 * (values[1, 0] + values[0, 1] * sine + values[1, 1] * cosine)
    return jnp.concatenate([real_part, other_part], axis=0)


def to_channels(stacked):
    return lax.all_to_all(
        jnp.swapaxes(stacked, 1, 2)[:, :, None, :], "inner", split_axis=1, concat_axis=2, tiled=True
    )


def to_positions(values):
    moved = lax.all_to_all(values, "inner", split_axis=2, concat_axis=1, tiled=True)
    return jnp.swapaxes(moved[:, :, 0, :], 1, 2)


def filter_features(places, seq_total, bands):
    columns = [places.astype(jnp.float32) / seq_total]
    for band in range(bands):
        stride = min(2**band, seq_total // 4)
        phases = places % (seq_total // stride) * stride
        angles = full_turn / seq_total * phases.astype(jnp.float32)
        columns.append(jnp.cos(angles))
        columns.append(jnp.sin(angles))
    return jnp.stack(columns, axis=1)


def decay_window(rates, places):
    return jnp.exp(-rates * places.astype(jnp.float32)) * jnp.sqrt(-jnp.expm1(-2.0 * rates))


def body(projected, short_weight, filter_in, filter_bias, filter_out, filter_decay, cotangent):
    parts = lax.axis_size("inner")
    inner_id = lax.axis_index("inner")
    length = projected.shape[0]
    chans = projected.shape[2]
    taps = short_weight.shape[0]
    bands = (filter_in.shape[0] - 1) // 2
    seq_total = parts * length
    slices = chans // parts
    earlier = passed_along(projected[length - taps + 1 :], "inner", 1)
    extended = jnp.concatenate([earlier, projected], axis=0)
    mixed = jnp.zeros((length, 3, chans), jnp.float32)
    for offset in range(taps):
        mixed = (
            mixed + short_weight[offset] * extended[taps - 1 - offset : taps - 1 - offset + length]
        )
    query = mixed[:, 0]
    key_part = mixed[:, 1]
    value_part = mixed[:, 2]
    product = key_part * value_part
    grad_conv = cotangent * query
    places = inner_id * length + jnp.arange(length, dtype=jnp.int32)
    activity = jnp.sin(
        jnp.dot(filter_features(places, seq_total, bands), filter_in, precision=exact_mode)
        + filter_bias
    )
    shaped = jnp.dot(activity, filter_out, precision=exact_mode)
    long_filter = shaped * decay_window(filter_decay[None, :], places[:, None])
    moved = to_channels(jnp.stack([product, long_filter, grad_conv]))
    signal_rows = moved[0]
    filter_rows = moved[1]
    grad_rows = moved[2]
    spectra = forward_padded(jnp.concatenate([signal_rows, filter_rows, grad_rows], axis=0))
    signal_spec = spectra[:, :, :slices]
    filter_spec = spectra[:, :, slices : 2 * slices]
    grad_spec = spectra[:, :, 2 * slices :]
    paired = jnp.concatenate(
        [
            times_complex(signal_spec, filter_spec),
            times_complex(conjugate(filter_spec), grad_spec),
            times_complex(grad_spec, conjugate(signal_spec)),
        ],
        axis=2,
    )
    spread = slices // 2
    ordered = jnp.concatenate(
        [paired[:, :, : slices], paired[:, :, 2 * slices : 2 * slices + spread],
         paired[:, :, slices : 2 * slices], paired[:, :, 2 * slices + spread :]],
        axis=2,
    )
    returned = inverse_padded(ordered)
    returned = jnp.concatenate(
        [returned[:slices], returned[slices + spread : 2 * slices + spread],
         returned[slices : slices + spread], returned[2 * slices + spread :]],
        axis=0,
    )
    back = to_positions(returned.reshape(3, slices, parts, length))
    conv = back[0]
    grad_product = back[1]
    grad_filter = back[2] / math.sqrt(seq_total)
    operator_out = (query * conv).astype(jnp.bfloat16)
    grad_query = cotangent * conv
    grad_mixed = jnp.stack([grad_query, grad_product * value_part, grad_product * key_part], axis=1)
    later = passed_along(grad_mixed[: taps - 1], "inner", -1)
    tailed = jnp.concatenate([grad_mixed, later], axis=0)
    grad_projected = jnp.zeros((length, 3, chans), jnp.float32)
    for offset in range(taps):
        grad_projected = grad_projected + short_weight[offset] * tailed[offset : offset + length]
    return (operator_out, grad_projected.astype(jnp.bfloat16), grad_filter)


def solution(mesh):
    in_specs = (
        P("inner", None, "outer"),
        P(None, None, "outer"),
        P(),
        P(),
        P(None, "outer"),
        P("outer"),
        P("inner", "outer"),
    )
    out_specs = (P("inner", "outer"), P("inner", None, "outer"), P("inner", "outer"))
    return jax.shard_map(body, mesh=mesh, in_specs=in_specs, out_specs=out_specs, check_vma=False)
```

```python
import math

import jax
import numpy as np
import jax.numpy as jnp
from jax import lax
from jax.sharding import PartitionSpec as P

exact_mode = lax.Precision.HIGHEST
transform_mode = lax.Precision.HIGH
full_turn = 6.283185307179586


def passed_along(value, axis, by):
    length = lax.axis_size(axis)
    pairs = [(i, i + by) for i in range(length) if 0 <= i + by < length]
    return lax.ppermute(value, axis, pairs)


def turning(numbers, period, direction):
    angles = direction * full_turn / period * (numbers % period).astype(np.float64)
    return (jnp.asarray(np.cos(angles), jnp.float32), jnp.asarray(np.sin(angles), jnp.float32))


def rotate(values, cosine, sine):
    return jnp.stack([values[0] * cosine - values[1] * sine, values[0] * sine + values[1] * cosine])


def times_complex(first, second):
    return jnp.stack(
        [first[0] * second[0] - first[1] * second[1], first[0] * second[1] + first[1] * second[0]]
    )


def conjugate(values):
    return jnp.stack([values[0], -values[1]])


def mix_axis(values, count, direction, pattern):
    index = np.arange(count, dtype=np.int64)
    cosine, sine = turning(index[:, None] * index[None, :], count, direction)
    matrix = jnp.stack([jnp.stack([cosine, -sine]), jnp.stack([sine, cosine])])
    pair, result = pattern.split("->")
    table, operand = pair.split(",")
    joined = "zy" + table + ",y" + operand + "->z" + result
    return jnp.einsum(joined, matrix, values, precision=transform_mode)


def grid_places(parts, length):
    return (
        np.arange(parts, dtype=np.int64)[:, None] * length
        + np.arange(length, dtype=np.int64)[None, :]
    )


def forward_padded(signal):
    parts = signal.shape[1]
    length = signal.shape[2]
    seq_total = parts * length
    cosine, sine = turning(grid_places(parts, length), 2 * seq_total, -1.0)
    values = jnp.stack(
        [jnp.stack([signal, signal * cosine]), jnp.stack([jnp.zeros_like(signal), signal * sine])]
    )
    values = mix_axis(values, parts, -1.0, "ap,hrpj->hraj")
    index_a = np.arange(parts, dtype=np.int64)[:, None]
    index_j = np.arange(length, dtype=np.int64)[None, :]
    cosine, sine = turning(index_a * index_j, seq_total, -1.0)
    values = rotate(values, cosine, sine)
    return mix_axis(values, length, -1.0, "bj,hraj->hrab")


def inverse_padded(spectrum):
    half = spectrum.shape[2] // 2
    first = spectrum[:, :, :half]
    second = spectrum[:, :, half:]
    joined = jnp.stack([first[0] - second[1], first[1] + second[0]])
    parts = spectrum.shape[3]
    length = spectrum.shape[4]
    seq_total = parts * length
    values = mix_axis(joined, length, 1.0, "jb,hrab->hraj")
    index_a = np.arange(parts, dtype=np.int64)[:, None]
    index_j = np.arange(length, dtype=np.int64)[None, :]
    cosine, sine = turning(index_a * index_j, seq_total, 1.0)
    values = rotate(values, cosine, sine)
    values = mix_axis(values, parts, 1.0, "pa,hraj->hrpj") / seq_total
    cosine, sine = turning(grid_places(parts, length), 2 * seq_total, 1.0)
    real_part = 0.5 * (values[0, 0] + values[0, 1] * cosine - values[1, 1] * sine)
    other_part = 0.5 * (values[1, 0] + values[0, 1] * sine + values[1, 1] * cosine)
    return jnp.concatenate([real_part, other_part], axis=0)


def to_channels(stacked):
    return lax.all_to_all(
        jnp.swapaxes(stacked, 1, 2)[:, :, None, :], "inner", split_axis=1, concat_axis=2, tiled=True
    )


def to_positions(values):
    moved = lax.all_to_all(values, "inner", split_axis=2, concat_axis=1, tiled=True)
    return jnp.swapaxes(moved[:, :, 0, :], 1, 2)


def filter_features(places, seq_total, bands):
    columns = [places.astype(jnp.float32) / seq_total]
    for band in range(bands):
        stride = min(2**band, seq_total // 4)
        phases = places % (seq_total // stride) * stride
        angles = full_turn / seq_total * phases.astype(jnp.float32)
        columns.append(jnp.cos(angles))
        columns.append(jnp.sin(angles))
    return jnp.stack(columns, axis=1)


def decay_window(rates, places):
    return jnp.exp(-rates * places.astype(jnp.float32)) * jnp.sqrt(-jnp.expm1(-2.0 * rates))


def body(projected, short_weight, filter_in, filter_bias, filter_out, filter_decay, cotangent):
    parts = lax.axis_size("inner")
    inner_id = lax.axis_index("inner")
    length = projected.shape[0]
    chans = projected.shape[2]
    taps = short_weight.shape[0]
    bands = (filter_in.shape[0] - 1) // 2
    seq_total = parts * length
    slices = chans // parts
    earlier = passed_along(projected[length - taps + 1 :], "inner", 1)
    extended = jnp.concatenate([earlier, projected], axis=0)
    mixed = jnp.zeros((length, 3, chans), jnp.float32)
    for offset in range(taps):
        mixed = (
            mixed + short_weight[offset] * extended[taps - 1 - offset : taps - 1 - offset + length]
        )
    query = mixed[:, 0]
    key_part = mixed[:, 1]
    value_part = mixed[:, 2]
    product = key_part * value_part
    grad_conv = cotangent * query
    places = inner_id * length + jnp.arange(length, dtype=jnp.int32)
    activity = jnp.sin(
        jnp.dot(filter_features(places, seq_total, bands), filter_in, precision=exact_mode)
        + filter_bias
    )
    shaped = jnp.dot(activity, filter_out, precision=exact_mode)
    long_filter = shaped * decay_window(filter_decay[None, :], places[:, None])
    moved = to_channels(jnp.stack([product, long_filter, grad_conv]))
    signal_rows = moved[0]
    filter_rows = moved[1]
    grad_rows = moved[2]
    spectra = forward_padded(jnp.concatenate([signal_rows, filter_rows, grad_rows], axis=0))
    signal_spec = spectra[:, :, :slices]
    filter_spec = spectra[:, :, slices : 2 * slices]
    grad_spec = spectra[:, :, 2 * slices :]
    paired = jnp.concatenate(
        [
            times_complex(signal_spec, filter_spec),
            times_complex(conjugate(filter_spec), grad_spec),
            times_complex(grad_spec, conjugate(signal_spec)),
        ],
        axis=2,
    )
    spread = slices // 2
    ordered = jnp.concatenate(
        [paired[:, :, : slices], paired[:, :, 2 * slices : 2 * slices + spread],
         paired[:, :, slices : 2 * slices], paired[:, :, 2 * slices + spread :]],
        axis=2,
    )
    returned = inverse_padded(ordered)
    returned = jnp.concatenate(
        [returned[:slices], returned[slices + spread : 2 * slices + spread],
         returned[slices : slices + spread], returned[2 * slices + spread :]],
        axis=0,
    )
    back = to_positions(returned.reshape(3, slices, parts, length))
    conv = back[0]
    grad_product = back[1]
    grad_filter = back[2] / math.sqrt(seq_total)
    operator_out = (query * conv).astype(jnp.bfloat16)
    grad_query = cotangent * conv
    grad_mixed = jnp.stack([grad_query, grad_product * value_part, grad_product * key_part], axis=1)
    later = passed_along(grad_mixed[: taps - 1], "inner", -1)
    tailed = jnp.concatenate([grad_mixed, later], axis=0)
    grad_projected = jnp.zeros((length, 3, chans), jnp.float32)
    for offset in range(taps):
        grad_projected = grad_projected + short_weight[offset] * tailed[offset : offset + length]
    return (operator_out, grad_projected.astype(jnp.bfloat16), grad_filter)


def solution(mesh):
    in_specs = (
        P("inner", None, "outer"),
        P(None, None, "outer"),
        P(),
        P(),
        P(None, "outer"),
        P("outer"),
        P("inner", "outer"),
    )
    out_specs = (P("inner", "outer"), P("inner", None, "outer"), P("inner", "outer"))
    return jax.shard_map(body, mesh=mesh, in_specs=in_specs, out_specs=out_specs, check_vma=False)
```

```python
import math

import jax
import numpy as np
import jax.numpy as jnp
from jax import lax
from jax.sharding import PartitionSpec as P

exact_mode = lax.Precision.HIGHEST
transform_mode = lax.Precision.HIGH
full_turn = 6.283185307179586


def passed_along(value, axis, by):
    length = lax.axis_size(axis)
    pairs = [(i, i + by) for i in range(length) if 0 <= i + by < length]
    return lax.ppermute(value, axis, pairs)


def turning(numbers, period, direction):
    angles = direction * full_turn / period * (numbers % period).astype(np.float64)
    return (jnp.asarray(np.cos(angles), jnp.float32), jnp.asarray(np.sin(angles), jnp.float32))


def rotate(values, cosine, sine):
    return jnp.stack([values[0] * cosine - values[1] * sine, values[0] * sine + values[1] * cosine])


def times_complex(first, second):
    return jnp.stack(
        [first[0] * second[0] - first[1] * second[1], first[0] * second[1] + first[1] * second[0]]
    )


def conjugate(values):
    return jnp.stack([values[0], -values[1]])


def mix_axis(values, count, direction, pattern):
    index = np.arange(count, dtype=np.int64)
    cosine, sine = turning(index[:, None] * index[None, :], count, direction)
    matrix = jnp.stack([jnp.stack([cosine, -sine]), jnp.stack([sine, cosine])])
    pair, result = pattern.split("->")
    table, operand = pair.split(",")
    joined = "zy" + table + ",y" + operand + "->z" + result
    return jnp.einsum(joined, matrix, values, precision=transform_mode)


def grid_places(parts, length):
    return (
        np.arange(parts, dtype=np.int64)[:, None] * length
        + np.arange(length, dtype=np.int64)[None, :]
    )


def forward_padded(signal):
    parts = signal.shape[1]
    length = signal.shape[2]
    seq_total = parts * length
    cosine, sine = turning(grid_places(parts, length), 2 * seq_total, -1.0)
    values = jnp.stack(
        [jnp.stack([signal, signal * cosine]), jnp.stack([jnp.zeros_like(signal), signal * sine])]
    )
    values = mix_axis(values, parts, -1.0, "ap,hrpj->hraj")
    index_a = np.arange(parts, dtype=np.int64)[:, None]
    index_j = np.arange(length, dtype=np.int64)[None, :]
    cosine, sine = turning(index_a * index_j, seq_total, -1.0)
    values = rotate(values, cosine, sine)
    return mix_axis(values, length, -1.0, "bj,hraj->hrab")


def inverse_padded(spectrum):
    half = spectrum.shape[2] // 2
    first = spectrum[:, :, :half]
    second = spectrum[:, :, half:]
    joined = jnp.stack([first[0] - second[1], first[1] + second[0]])
    parts = spectrum.shape[3]
    length = spectrum.shape[4]
    seq_total = parts * length
    values = mix_axis(joined, length, 1.0, "jb,hrab->hraj")
    index_a = np.arange(parts, dtype=np.int64)[:, None]
    index_j = np.arange(length, dtype=np.int64)[None, :]
    cosine, sine = turning(index_a * index_j, seq_total, 1.0)
    values = rotate(values, cosine, sine)
    values = mix_axis(values, parts, 1.0, "pa,hraj->hrpj") / seq_total
    cosine, sine = turning(grid_places(parts, length), 2 * seq_total, 1.0)
    real_part = 0.5 * (values[0, 0] + values[0, 1] * cosine - values[1, 1] * sine)
    other_part = 0.5 * (values[1, 0] + values[0, 1] * sine + values[1, 1] * cosine)
    return jnp.concatenate([real_part, other_part], axis=0)


def to_channels(stacked):
    return lax.all_to_all(
        jnp.swapaxes(stacked, 1, 2)[:, :, None, :], "inner", split_axis=1, concat_axis=2, tiled=True
    )


def to_positions(values):
    moved = lax.all_to_all(values, "inner", split_axis=2, concat_axis=1, tiled=True)
    return jnp.swapaxes(moved[:, :, 0, :], 1, 2)


def filter_features(places, seq_total, bands):
    columns = [places.astype(jnp.float32) / seq_total]
    for band in range(bands):
        stride = min(2**band, seq_total // 4)
        phases = places % (seq_total // stride) * stride
        angles = full_turn / seq_total * phases.astype(jnp.float32)
        columns.append(jnp.cos(angles))
        columns.append(jnp.sin(angles))
    return jnp.stack(columns, axis=1)


def decay_window(rates, places):
    return jnp.exp(-rates * places.astype(jnp.float32)) * jnp.sqrt(-jnp.expm1(-2.0 * rates))


def split_wide(values):
    rounded = lax.reduce_precision(values, exponent_bits=8, mantissa_bits=7)
    return rounded.astype(jnp.bfloat16), (values - rounded).astype(jnp.bfloat16)


def body(projected, short_weight, filter_in, filter_bias, filter_out, filter_decay, cotangent):
    parts = lax.axis_size("inner")
    inner_id = lax.axis_index("inner")
    length = projected.shape[0]
    chans = projected.shape[2]
    taps = short_weight.shape[0]
    bands = (filter_in.shape[0] - 1) // 2
    seq_total = parts * length
    slices = chans // parts
    places = inner_id * length + jnp.arange(length, dtype=jnp.int32)
    activity = jnp.sin(
        jnp.dot(filter_features(places, seq_total, bands), filter_in, precision=exact_mode)
        + filter_bias
    )
    shaped = jnp.dot(activity, filter_out, precision=exact_mode)
    long_filter = shaped * decay_window(filter_decay[None, :], places[:, None])
    filter_upper, filter_lower = split_wide(long_filter)
    outgoing = jnp.stack(
        [projected[:, 0], projected[:, 1], projected[:, 2], cotangent, filter_upper, filter_lower]
    )
    moved = to_channels(outgoing).reshape(6, slices, seq_total)
    first = inner_id * slices
    weights = lax.dynamic_slice_in_dim(short_weight, first, slices, axis=2)[:, :, :, None]
    mixed = []
    for group in range(3):
        padded = jnp.pad(moved[group], ((0, 0), (taps - 1, 0)))
        total = jnp.zeros((slices, seq_total), jnp.float32)
        for offset in range(taps):
            total = total + weights[offset, group] * padded[
                :, taps - 1 - offset : taps - 1 - offset + seq_total
            ]
        mixed.append(total)
    query, key_part, value_part = mixed
    product = key_part * value_part
    grad_conv = moved[3] * query
    long_rows = moved[4].astype(jnp.float32) + moved[5].astype(jnp.float32)
    signal_rows = product.reshape(slices, parts, length)
    filter_rows = long_rows.reshape(slices, parts, length)
    grad_rows = grad_conv.reshape(slices, parts, length)
    spectra = forward_padded(jnp.concatenate([signal_rows, filter_rows, grad_rows], axis=0))
    signal_spec = spectra[:, :, :slices]
    filter_spec = spectra[:, :, slices : 2 * slices]
    grad_spec = spectra[:, :, 2 * slices :]
    paired = jnp.concatenate(
        [
            times_complex(signal_spec, filter_spec),
            times_complex(conjugate(filter_spec), grad_spec),
            times_complex(grad_spec, conjugate(signal_spec)),
        ],
        axis=2,
    )
    spread = slices // 2
    ordered = jnp.concatenate(
        [paired[:, :, : slices], paired[:, :, 2 * slices : 2 * slices + spread],
         paired[:, :, slices : 2 * slices], paired[:, :, 2 * slices + spread :]],
        axis=2,
    )
    returned = inverse_padded(ordered)
    returned = jnp.concatenate(
        [returned[:slices], returned[slices + spread : 2 * slices + spread],
         returned[slices : slices + spread], returned[2 * slices + spread :]],
        axis=0,
    ).reshape(3, slices, seq_total)
    conv = returned[0]
    grad_product = returned[1]
    grad_filter = returned[2] / math.sqrt(seq_total)
    operator_out = (query * conv).astype(jnp.bfloat16)
    grad_mixed = [moved[3] * conv, grad_product * value_part, grad_product * key_part]
    grad_projected = []
    for group in range(3):
        padded = jnp.pad(grad_mixed[group], ((0, 0), (0, taps - 1)))
        total = jnp.zeros((slices, seq_total), jnp.float32)
        for offset in range(taps):
            total = total + weights[offset, group] * padded[:, offset : offset + seq_total]
        grad_projected.append(total.astype(jnp.bfloat16))
    grad_upper, grad_lower = split_wide(grad_filter)
    back = to_positions(
        jnp.stack([operator_out] + grad_projected + [grad_upper, grad_lower]).reshape(
            6, slices, parts, length
        )
    )
    grad_out = back[4].astype(jnp.float32) + back[5].astype(jnp.float32)
    return (back[0], jnp.stack([back[1], back[2], back[3]], axis=1), grad_out)


def solution(mesh):
    in_specs = (
        P("inner", None, "outer"),
        P(None, None, "outer"),
        P(),
        P(),
        P(None, "outer"),
        P("outer"),
        P("inner", "outer"),
    )
    out_specs = (P("inner", "outer"), P("inner", None, "outer"), P("inner", "outer"))
    return jax.shard_map(body, mesh=mesh, in_specs=in_specs, out_specs=out_specs, check_vma=False)
```

```python
import math

import jax
import numpy as np
import jax.numpy as jnp
from jax import lax
from jax.sharding import PartitionSpec as P

exact_mode = lax.Precision.HIGHEST
transform_mode = lax.Precision.HIGH
full_turn = 6.283185307179586


def passed_along(value, axis, by):
    length = lax.axis_size(axis)
    pairs = [(i, i + by) for i in range(length) if 0 <= i + by < length]
    return lax.ppermute(value, axis, pairs)


def turning(numbers, period, direction):
    angles = direction * full_turn / period * (numbers % period).astype(np.float64)
    return (jnp.asarray(np.cos(angles), jnp.float32), jnp.asarray(np.sin(angles), jnp.float32))


def rotate(values, cosine, sine):
    return jnp.stack([values[0] * cosine - values[1] * sine, values[0] * sine + values[1] * cosine])


def times_complex(first, second):
    return jnp.stack(
        [first[0] * second[0] - first[1] * second[1], first[0] * second[1] + first[1] * second[0]]
    )


def conjugate(values):
    return jnp.stack([values[0], -values[1]])


def mix_axis(values, count, direction, pattern):
    index = np.arange(count, dtype=np.int64)
    cosine, sine = turning(index[:, None] * index[None, :], count, direction)
    matrix = jnp.stack([jnp.stack([cosine, -sine]), jnp.stack([sine, cosine])])
    pair, result = pattern.split("->")
    table, operand = pair.split(",")
    joined = "zy" + table + ",y" + operand + "->z" + result
    return jnp.einsum(joined, matrix, values, precision=transform_mode)


def grid_places(parts, length):
    return (
        np.arange(parts, dtype=np.int64)[:, None] * length
        + np.arange(length, dtype=np.int64)[None, :]
    )


def forward_padded(signal):
    parts = signal.shape[1]
    length = signal.shape[2]
    seq_total = parts * length
    cosine, sine = turning(grid_places(parts, length), 2 * seq_total, -1.0)
    values = jnp.stack(
        [jnp.stack([signal, signal * cosine]), jnp.stack([jnp.zeros_like(signal), signal * sine])]
    )
    values = mix_axis(values, parts, -1.0, "ap,hrpj->hraj")
    index_a = np.arange(parts, dtype=np.int64)[:, None]
    index_j = np.arange(length, dtype=np.int64)[None, :]
    cosine, sine = turning(index_a * index_j, seq_total, -1.0)
    values = rotate(values, cosine, sine)
    return mix_axis(values, length, -1.0, "bj,hraj->hrab")


def inverse_padded(spectrum):
    half = spectrum.shape[2] // 2
    first = spectrum[:, :, :half]
    second = spectrum[:, :, half:]
    joined = jnp.stack([first[0] - second[1], first[1] + second[0]])
    parts = spectrum.shape[3]
    length = spectrum.shape[4]
    seq_total = parts * length
    values = mix_axis(joined, length, 1.0, "jb,hrab->hraj")
    index_a = np.arange(parts, dtype=np.int64)[:, None]
    index_j = np.arange(length, dtype=np.int64)[None, :]
    cosine, sine = turning(index_a * index_j, seq_total, 1.0)
    values = rotate(values, cosine, sine)
    values = mix_axis(values, parts, 1.0, "pa,hraj->hrpj") / seq_total
    cosine, sine = turning(grid_places(parts, length), 2 * seq_total, 1.0)
    real_part = 0.5 * (values[0, 0] + values[0, 1] * cosine - values[1, 1] * sine)
    other_part = 0.5 * (values[1, 0] + values[0, 1] * sine + values[1, 1] * cosine)
    return jnp.concatenate([real_part, other_part], axis=0)


def to_channels(stacked):
    return lax.all_to_all(
        jnp.swapaxes(stacked, 1, 2)[:, :, None, :], "inner", split_axis=1, concat_axis=2, tiled=True
    )


def to_positions(values):
    moved = lax.all_to_all(values, "inner", split_axis=2, concat_axis=1, tiled=True)
    return jnp.swapaxes(moved[:, :, 0, :], 1, 2)


def filter_features(places, seq_total, bands):
    columns = [places.astype(jnp.float32) / seq_total]
    for band in range(bands):
        stride = min(2**band, seq_total // 4)
        phases = places % (seq_total // stride) * stride
        angles = full_turn / seq_total * phases.astype(jnp.float32)
        columns.append(jnp.cos(angles))
        columns.append(jnp.sin(angles))
    return jnp.stack(columns, axis=1)


def decay_window(rates, places):
    return jnp.exp(-rates * places.astype(jnp.float32)) * jnp.sqrt(-jnp.expm1(-2.0 * rates))


def split_wide(values):
    rounded = lax.reduce_precision(values, exponent_bits=8, mantissa_bits=7)
    return rounded.astype(jnp.bfloat16), (values - rounded).astype(jnp.bfloat16)


def body(projected, short_weight, filter_in, filter_bias, filter_out, filter_decay, cotangent):
    parts = lax.axis_size("inner")
    inner_id = lax.axis_index("inner")
    length = projected.shape[0]
    chans = projected.shape[2]
    taps = short_weight.shape[0]
    bands = (filter_in.shape[0] - 1) // 2
    seq_total = parts * length
    slices = chans // parts
    places = inner_id * length + jnp.arange(length, dtype=jnp.int32)
    activity = jnp.sin(
        jnp.dot(filter_features(places, seq_total, bands), filter_in, precision=exact_mode)
        + filter_bias
    )
    shaped = jnp.dot(activity, filter_out, precision=exact_mode)
    long_filter = shaped * decay_window(filter_decay[None, :], places[:, None])
    filter_upper, filter_lower = split_wide(long_filter)
    outgoing = jnp.concatenate(
        [projected, cotangent[:, None], filter_upper[:, None], filter_lower[:, None]], axis=1
    )
    arrived = lax.all_to_all(
        outgoing.reshape(length, 6, parts, slices), "inner", split_axis=2, concat_axis=0, tiled=True
    )
    moved = jnp.transpose(arrived.reshape(seq_total, 6, slices), (1, 2, 0))
    first = inner_id * slices
    weights = lax.dynamic_slice_in_dim(short_weight, first, slices, axis=2)[:, :, :, None]
    mixed = []
    for group in range(3):
        padded = jnp.pad(moved[group], ((0, 0), (taps - 1, 0)))
        total = jnp.zeros((slices, seq_total), jnp.float32)
        for offset in range(taps):
            total = total + weights[offset, group] * padded[
                :, taps - 1 - offset : taps - 1 - offset + seq_total
            ]
        mixed.append(total)
    query, key_part, value_part = mixed
    product = key_part * value_part
    grad_conv = moved[3] * query
    long_rows = moved[4].astype(jnp.float32) + moved[5].astype(jnp.float32)
    signal_rows = product.reshape(slices, parts, length)
    filter_rows = long_rows.reshape(slices, parts, length)
    grad_rows = grad_conv.reshape(slices, parts, length)
    spectra = forward_padded(jnp.concatenate([signal_rows, filter_rows, grad_rows], axis=0))
    signal_spec = spectra[:, :, :slices]
    filter_spec = spectra[:, :, slices : 2 * slices]
    grad_spec = spectra[:, :, 2 * slices :]
    paired = jnp.concatenate(
        [
            times_complex(signal_spec, filter_spec),
            times_complex(conjugate(filter_spec), grad_spec),
            times_complex(grad_spec, conjugate(signal_spec)),
        ],
        axis=2,
    )
    spread = slices // 2
    ordered = jnp.concatenate(
        [paired[:, :, : slices], paired[:, :, 2 * slices : 2 * slices + spread],
         paired[:, :, slices : 2 * slices], paired[:, :, 2 * slices + spread :]],
        axis=2,
    )
    returned = inverse_padded(ordered)
    returned = jnp.concatenate(
        [returned[:slices], returned[slices + spread : 2 * slices + spread],
         returned[slices : slices + spread], returned[2 * slices + spread :]],
        axis=0,
    ).reshape(3, slices, seq_total)
    conv = returned[0]
    grad_product = returned[1]
    grad_filter = returned[2] / math.sqrt(seq_total)
    operator_out = (query * conv).astype(jnp.bfloat16)
    grad_mixed = [moved[3] * conv, grad_product * value_part, grad_product * key_part]
    grad_projected = []
    for group in range(3):
        padded = jnp.pad(grad_mixed[group], ((0, 0), (0, taps - 1)))
        total = jnp.zeros((slices, seq_total), jnp.float32)
        for offset in range(taps):
            total = total + weights[offset, group] * padded[:, offset : offset + seq_total]
        grad_projected.append(total.astype(jnp.bfloat16))
    grad_upper, grad_lower = split_wide(grad_filter)
    leaving = jnp.transpose(
        jnp.stack([operator_out] + grad_projected + [grad_upper, grad_lower]), (2, 0, 1)
    )
    back = lax.all_to_all(
        leaving.reshape(parts, length, 6, 1, slices), "inner", split_axis=0, concat_axis=3, tiled=True
    ).reshape(length, 6, chans)
    grad_out = back[:, 4].astype(jnp.float32) + back[:, 5].astype(jnp.float32)
    return (back[:, 0], back[:, 1:4], grad_out)


def solution(mesh):
    in_specs = (
        P("inner", None, "outer"),
        P(None, None, "outer"),
        P(),
        P(),
        P(None, "outer"),
        P("outer"),
        P("inner", "outer"),
    )
    out_specs = (P("inner", "outer"), P("inner", None, "outer"), P("inner", "outer"))
    return jax.shard_map(body, mesh=mesh, in_specs=in_specs, out_specs=out_specs, check_vma=False)
```

```python
import math

import jax
import numpy as np
import jax.numpy as jnp
from jax import lax
from jax.sharding import PartitionSpec as P

exact_mode = lax.Precision.HIGHEST
transform_mode = lax.Precision.HIGH
full_turn = 6.283185307179586


def passed_along(value, axis, by):
    length = lax.axis_size(axis)
    pairs = [(i, i + by) for i in range(length) if 0 <= i + by < length]
    return lax.ppermute(value, axis, pairs)


def turning(numbers, period, direction):
    angles = direction * full_turn / period * (numbers % period).astype(np.float64)
    return (jnp.asarray(np.cos(angles), jnp.float32), jnp.asarray(np.sin(angles), jnp.float32))


def rotate(values, cosine, sine):
    return jnp.stack([values[0] * cosine - values[1] * sine, values[0] * sine + values[1] * cosine])


def times_complex(first, second):
    return jnp.stack(
        [first[0] * second[0] - first[1] * second[1], first[0] * second[1] + first[1] * second[0]]
    )


def conjugate(values):
    return jnp.stack([values[0], -values[1]])


def mix_axis(values, count, direction, pattern):
    index = np.arange(count, dtype=np.int64)
    angles = -full_turn / count * ((index[:, None] * index[None, :]) % count).astype(np.float64)
    cosine, sine = np.cos(angles), np.sin(angles)
    matrix = jnp.asarray(np.stack([np.stack([cosine, -sine]), np.stack([sine, cosine])]), jnp.float32)
    pair, result = pattern.split("->")
    table, operand = pair.split(",")
    order = "zy" if direction < 0 else "yz"
    joined = order + table + ",y" + operand + "->z" + result
    return jnp.einsum(joined, matrix, values, precision=transform_mode)


def grid_places(parts, length):
    return (
        np.arange(parts, dtype=np.int64)[:, None] * length
        + np.arange(length, dtype=np.int64)[None, :]
    )


def forward_padded(signal):
    parts = signal.shape[1]
    length = signal.shape[2]
    seq_total = parts * length
    cosine, sine = turning(grid_places(parts, length), 2 * seq_total, -1.0)
    values = jnp.stack(
        [jnp.stack([signal, signal * cosine]), jnp.stack([jnp.zeros_like(signal), signal * sine])]
    )
    values = mix_axis(values, parts, -1.0, "ap,hrpj->hraj")
    index_a = np.arange(parts, dtype=np.int64)[:, None]
    index_j = np.arange(length, dtype=np.int64)[None, :]
    cosine, sine = turning(index_a * index_j, seq_total, -1.0)
    values = rotate(values, cosine, sine)
    return mix_axis(values, length, -1.0, "bj,hraj->hrab")


def inverse_padded(spectrum):
    half = spectrum.shape[2] // 2
    first = spectrum[:, :, :half]
    second = spectrum[:, :, half:]
    joined = jnp.stack([first[0] - second[1], first[1] + second[0]])
    parts = spectrum.shape[3]
    length = spectrum.shape[4]
    seq_total = parts * length
    values = mix_axis(joined, length, 1.0, "jb,hrab->hraj")
    index_a = np.arange(parts, dtype=np.int64)[:, None]
    index_j = np.arange(length, dtype=np.int64)[None, :]
    cosine, sine = turning(index_a * index_j, seq_total, -1.0)
    values = jnp.stack(
        [values[0] * cosine + values[1] * sine, values[1] * cosine - values[0] * sine]
    )
    values = mix_axis(values, parts, 1.0, "pa,hraj->hrpj") / seq_total
    cosine, sine = turning(grid_places(parts, length), 2 * seq_total, -1.0)
    real_part = 0.5 * (values[0, 0] + values[0, 1] * cosine + values[1, 1] * sine)
    other_part = 0.5 * (values[1, 0] - values[0, 1] * sine + values[1, 1] * cosine)
    return jnp.concatenate([real_part, other_part], axis=0)


def to_channels(stacked):
    return lax.all_to_all(
        jnp.swapaxes(stacked, 1, 2)[:, :, None, :], "inner", split_axis=1, concat_axis=2, tiled=True
    )


def to_positions(values):
    moved = lax.all_to_all(values, "inner", split_axis=2, concat_axis=1, tiled=True)
    return jnp.swapaxes(moved[:, :, 0, :], 1, 2)


def filter_features(places, seq_total, bands):
    columns = [places.astype(jnp.float32) / seq_total]
    for band in range(bands):
        stride = min(2**band, seq_total // 4)
        phases = places % (seq_total // stride) * stride
        angles = full_turn / seq_total * phases.astype(jnp.float32)
        columns.append(jnp.cos(angles))
        columns.append(jnp.sin(angles))
    return jnp.stack(columns, axis=1)


def decay_window(rates, places):
    return jnp.exp(-rates * places.astype(jnp.float32)) * jnp.sqrt(-jnp.expm1(-2.0 * rates))


def split_wide(values):
    rounded = lax.reduce_precision(values, exponent_bits=8, mantissa_bits=7)
    return rounded.astype(jnp.bfloat16), (values - rounded).astype(jnp.bfloat16)


def body(projected, short_weight, filter_in, filter_bias, filter_out, filter_decay, cotangent):
    parts = lax.axis_size("inner")
    inner_id = lax.axis_index("inner")
    length = projected.shape[0]
    chans = projected.shape[2]
    taps = short_weight.shape[0]
    bands = (filter_in.shape[0] - 1) // 2
    seq_total = parts * length
    slices = chans // parts
    places = inner_id * length + jnp.arange(length, dtype=jnp.int32)
    activity = jnp.sin(
        jnp.dot(filter_features(places, seq_total, bands), filter_in, precision=exact_mode)
        + filter_bias
    )
    shaped = jnp.dot(activity, filter_out, precision=exact_mode)
    long_filter = shaped * decay_window(filter_decay[None, :], places[:, None])
    filter_upper, filter_lower = split_wide(long_filter)
    outgoing = jnp.concatenate(
        [projected, cotangent[:, None], filter_upper[:, None], filter_lower[:, None]], axis=1
    )
    arrived = lax.all_to_all(
        outgoing.reshape(length, 6, parts, slices), "inner", split_axis=2, concat_axis=0, tiled=True
    )
    moved = jnp.transpose(arrived.reshape(seq_total, 6, slices), (1, 2, 0))
    first = inner_id * slices
    weights = lax.dynamic_slice_in_dim(short_weight, first, slices, axis=2)[:, :, :, None]
    mixed = []
    for group in range(3):
        padded = jnp.pad(moved[group], ((0, 0), (taps - 1, 0)))
        total = jnp.zeros((slices, seq_total), jnp.float32)
        for offset in range(taps):
            total = total + weights[offset, group] * padded[
                :, taps - 1 - offset : taps - 1 - offset + seq_total
            ]
        mixed.append(total)
    query, key_part, value_part = mixed
    product = key_part * value_part
    grad_conv = moved[3] * query
    long_rows = moved[4].astype(jnp.float32) + moved[5].astype(jnp.float32)
    signal_rows = product.reshape(slices, parts, length)
    filter_rows = long_rows.reshape(slices, parts, length)
    grad_rows = grad_conv.reshape(slices, parts, length)
    spectra = forward_padded(jnp.concatenate([signal_rows, filter_rows, grad_rows], axis=0))
    signal_spec = spectra[:, :, :slices]
    filter_spec = spectra[:, :, slices : 2 * slices]
    grad_spec = spectra[:, :, 2 * slices :]
    paired = jnp.concatenate(
        [
            times_complex(signal_spec, filter_spec),
            times_complex(conjugate(filter_spec), grad_spec),
            times_complex(grad_spec, conjugate(signal_spec)),
        ],
        axis=2,
    )
    spread = slices // 2
    ordered = jnp.concatenate(
        [paired[:, :, : slices], paired[:, :, 2 * slices : 2 * slices + spread],
         paired[:, :, slices : 2 * slices], paired[:, :, 2 * slices + spread :]],
        axis=2,
    )
    returned = inverse_padded(ordered)
    returned = jnp.concatenate(
        [returned[:slices], returned[slices + spread : 2 * slices + spread],
         returned[slices : slices + spread], returned[2 * slices + spread :]],
        axis=0,
    ).reshape(3, slices, seq_total)
    conv = returned[0]
    grad_product = returned[1]
    grad_filter = returned[2] / math.sqrt(seq_total)
    operator_out = (query * conv).astype(jnp.bfloat16)
    grad_mixed = [moved[3] * conv, grad_product * value_part, grad_product * key_part]
    grad_projected = []
    for group in range(3):
        padded = jnp.pad(grad_mixed[group], ((0, 0), (0, taps - 1)))
        total = jnp.zeros((slices, seq_total), jnp.float32)
        for offset in range(taps):
            total = total + weights[offset, group] * padded[:, offset : offset + seq_total]
        grad_projected.append(total.astype(jnp.bfloat16))
    grad_upper, grad_lower = split_wide(grad_filter)
    leaving = jnp.transpose(
        jnp.stack([operator_out] + grad_projected + [grad_upper, grad_lower]), (2, 0, 1)
    )
    back = lax.all_to_all(
        leaving.reshape(parts, length, 6, 1, slices), "inner", split_axis=0, concat_axis=3, tiled=True
    ).reshape(length, 6, chans)
    grad_out = back[:, 4].astype(jnp.float32) + back[:, 5].astype(jnp.float32)
    return (back[:, 0], back[:, 1:4], grad_out)


def solution(mesh):
    in_specs = (
        P("inner", None, "outer"),
        P(None, None, "outer"),
        P(),
        P(),
        P(None, "outer"),
        P("outer"),
        P("inner", "outer"),
    )
    out_specs = (P("inner", "outer"), P("inner", None, "outer"), P("inner", "outer"))
    return jax.shard_map(body, mesh=mesh, in_specs=in_specs, out_specs=out_specs, check_vma=False)
```

```python
import math

import jax
import numpy as np
import jax.numpy as jnp
from jax import lax
from jax.sharding import PartitionSpec as P

exact_mode = lax.Precision.HIGHEST
transform_mode = lax.Precision.HIGH
full_turn = 6.283185307179586


def passed_along(value, axis, by):
    length = lax.axis_size(axis)
    pairs = [(i, i + by) for i in range(length) if 0 <= i + by < length]
    return lax.ppermute(value, axis, pairs)


def turning(numbers, period, direction):
    angles = direction * full_turn / period * (numbers % period).astype(np.float64)
    return (jnp.asarray(np.cos(angles), jnp.float32), jnp.asarray(np.sin(angles), jnp.float32))


def rotate(values, cosine, sine):
    return jnp.stack([values[0] * cosine - values[1] * sine, values[0] * sine + values[1] * cosine])


def times_complex(first, second):
    return jnp.stack(
        [first[0] * second[0] - first[1] * second[1], first[0] * second[1] + first[1] * second[0]]
    )


def conjugate(values):
    return jnp.stack([values[0], -values[1]])


def mix_axis(values, count, direction, pattern):
    index = np.arange(count, dtype=np.int64)
    angles = -full_turn / count * ((index[:, None] * index[None, :]) % count).astype(np.float64)
    cosine, sine = np.cos(angles), np.sin(angles)
    matrix = jnp.asarray(np.stack([np.stack([cosine, -sine]), np.stack([sine, cosine])]), jnp.float32)
    pair, result = pattern.split("->")
    table, operand = pair.split(",")
    order = "zy" if direction < 0 else "yz"
    joined = order + table + ",y" + operand + "->z" + result
    return jnp.einsum(joined, matrix, values, precision=transform_mode)


def grid_places(parts, length):
    return (
        np.arange(parts, dtype=np.int64)[:, None] * length
        + np.arange(length, dtype=np.int64)[None, :]
    )


def forward_padded(signal):
    parts = signal.shape[1]
    length = signal.shape[2]
    seq_total = parts * length
    cosine, sine = turning(grid_places(parts, length), 2 * seq_total, -1.0)
    values = jnp.stack(
        [jnp.stack([signal, signal * cosine]), jnp.stack([jnp.zeros_like(signal), signal * sine])]
    )
    values = mix_axis(values, parts, -1.0, "ap,hrpj->hraj")
    index_a = np.arange(parts, dtype=np.int64)[:, None]
    index_j = np.arange(length, dtype=np.int64)[None, :]
    cosine, sine = turning(index_a * index_j, seq_total, -1.0)
    values = rotate(values, cosine, sine)
    return mix_axis(values, length, -1.0, "bj,hraj->hrab")


def inverse_padded(spectrum):
    half = spectrum.shape[2] // 2
    first = spectrum[:, :, :half]
    second = spectrum[:, :, half:]
    joined = jnp.stack([first[0] - second[1], first[1] + second[0]])
    parts = spectrum.shape[3]
    length = spectrum.shape[4]
    seq_total = parts * length
    values = mix_axis(joined, length, 1.0, "jb,hrab->hraj")
    index_a = np.arange(parts, dtype=np.int64)[:, None]
    index_j = np.arange(length, dtype=np.int64)[None, :]
    cosine, sine = turning(index_a * index_j, seq_total, -1.0)
    values = jnp.stack(
        [values[0] * cosine + values[1] * sine, values[1] * cosine - values[0] * sine]
    )
    values = mix_axis(values, parts, 1.0, "pa,hraj->hrpj") / seq_total
    cosine, sine = turning(grid_places(parts, length), 2 * seq_total, -1.0)
    real_part = 0.5 * (values[0, 0] + values[0, 1] * cosine + values[1, 1] * sine)
    other_part = 0.5 * (values[1, 0] - values[0, 1] * sine + values[1, 1] * cosine)
    return jnp.concatenate([real_part, other_part], axis=0)


def to_channels(stacked):
    return lax.all_to_all(
        jnp.swapaxes(stacked, 1, 2)[:, :, None, :], "inner", split_axis=1, concat_axis=2, tiled=True
    )


def to_positions(values):
    moved = lax.all_to_all(values, "inner", split_axis=2, concat_axis=1, tiled=True)
    return jnp.swapaxes(moved[:, :, 0, :], 1, 2)


def filter_features(places, seq_total, bands):
    columns = [places.astype(jnp.float32) / seq_total]
    for band in range(bands):
        stride = min(2**band, seq_total // 4)
        phases = places % (seq_total // stride) * stride
        angles = full_turn / seq_total * phases.astype(jnp.float32)
        columns.append(jnp.cos(angles))
        columns.append(jnp.sin(angles))
    return jnp.stack(columns, axis=1)


def decay_window(rates, places):
    return jnp.exp(-rates * places.astype(jnp.float32)) * jnp.sqrt(-jnp.expm1(-2.0 * rates))


def split_wide(values):
    rounded = lax.reduce_precision(values, exponent_bits=8, mantissa_bits=7)
    return rounded.astype(jnp.bfloat16), (values - rounded).astype(jnp.bfloat16)


def body(projected, short_weight, filter_in, filter_bias, filter_out, filter_decay, cotangent):
    parts = lax.axis_size("inner")
    inner_id = lax.axis_index("inner")
    length = projected.shape[0]
    chans = projected.shape[2]
    taps = short_weight.shape[0]
    bands = (filter_in.shape[0] - 1) // 2
    seq_total = parts * length
    slices = chans // parts
    places = inner_id * length + jnp.arange(length, dtype=jnp.int32)
    activity = jnp.sin(
        jnp.dot(filter_features(places, seq_total, bands), filter_in, precision=exact_mode)
        + filter_bias
    )
    shaped = jnp.dot(activity, filter_out, precision=exact_mode)
    long_filter = shaped * decay_window(filter_decay[None, :], places[:, None])
    filter_upper, filter_lower = split_wide(long_filter)
    outgoing = jnp.concatenate(
        [projected, cotangent[:, None], filter_upper[:, None], filter_lower[:, None]], axis=1
    )
    outgoing = lax.optimization_barrier(outgoing)
    arrived = lax.all_to_all(
        outgoing.reshape(length, 6, parts, slices), "inner", split_axis=2, concat_axis=0, tiled=True
    )
    moved = jnp.transpose(arrived.reshape(seq_total, 6, slices), (1, 2, 0))
    first = inner_id * slices
    weights = lax.dynamic_slice_in_dim(short_weight, first, slices, axis=2)[:, :, :, None]
    mixed = []
    for group in range(3):
        padded = jnp.pad(moved[group], ((0, 0), (taps - 1, 0)))
        total = jnp.zeros((slices, seq_total), jnp.float32)
        for offset in range(taps):
            total = total + weights[offset, group] * padded[
                :, taps - 1 - offset : taps - 1 - offset + seq_total
            ]
        mixed.append(total)
    query, key_part, value_part = mixed
    product = key_part * value_part
    grad_conv = moved[3] * query
    long_rows = moved[4].astype(jnp.float32) + moved[5].astype(jnp.float32)
    signal_rows = product.reshape(slices, parts, length)
    filter_rows = long_rows.reshape(slices, parts, length)
    grad_rows = grad_conv.reshape(slices, parts, length)
    spectra = forward_padded(jnp.concatenate([signal_rows, filter_rows, grad_rows], axis=0))
    signal_spec = spectra[:, :, :slices]
    filter_spec = spectra[:, :, slices : 2 * slices]
    grad_spec = spectra[:, :, 2 * slices :]
    paired = jnp.concatenate(
        [
            times_complex(signal_spec, filter_spec),
            times_complex(conjugate(filter_spec), grad_spec),
            times_complex(grad_spec, conjugate(signal_spec)),
        ],
        axis=2,
    )
    spread = slices // 2
    ordered = jnp.concatenate(
        [paired[:, :, : slices], paired[:, :, 2 * slices : 2 * slices + spread],
         paired[:, :, slices : 2 * slices], paired[:, :, 2 * slices + spread :]],
        axis=2,
    )
    returned = inverse_padded(ordered)
    returned = jnp.concatenate(
        [returned[:slices], returned[slices + spread : 2 * slices + spread],
         returned[slices : slices + spread], returned[2 * slices + spread :]],
        axis=0,
    ).reshape(3, slices, seq_total)
    conv = returned[0]
    grad_product = returned[1]
    grad_filter = returned[2] / math.sqrt(seq_total)
    operator_out = (query * conv).astype(jnp.bfloat16)
    grad_mixed = [moved[3] * conv, grad_product * value_part, grad_product * key_part]
    grad_projected = []
    for group in range(3):
        padded = jnp.pad(grad_mixed[group], ((0, 0), (0, taps - 1)))
        total = jnp.zeros((slices, seq_total), jnp.float32)
        for offset in range(taps):
            total = total + weights[offset, group] * padded[:, offset : offset + seq_total]
        grad_projected.append(total.astype(jnp.bfloat16))
    grad_upper, grad_lower = split_wide(grad_filter)
    leaving = jnp.transpose(
        jnp.stack([operator_out] + grad_projected + [grad_upper, grad_lower]), (2, 0, 1)
    )
    back = lax.all_to_all(
        leaving.reshape(parts, length, 6, 1, slices), "inner", split_axis=0, concat_axis=3, tiled=True
    ).reshape(length, 6, chans)
    grad_out = back[:, 4].astype(jnp.float32) + back[:, 5].astype(jnp.float32)
    return (back[:, 0], back[:, 1:4], grad_out)


def solution(mesh):
    in_specs = (
        P("inner", None, "outer"),
        P(None, None, "outer"),
        P(),
        P(),
        P(None, "outer"),
        P("outer"),
        P("inner", "outer"),
    )
    out_specs = (P("inner", "outer"), P("inner", None, "outer"), P("inner", "outer"))
    return jax.shard_map(body, mesh=mesh, in_specs=in_specs, out_specs=out_specs, check_vma=False)
```

```python
import math

import jax
import numpy as np
import jax.numpy as jnp
from jax import lax
from jax.sharding import PartitionSpec as P

exact_mode = lax.Precision.HIGHEST
transform_mode = lax.Precision.HIGH
full_turn = 6.283185307179586


def passed_along(value, axis, by):
    length = lax.axis_size(axis)
    pairs = [(i, i + by) for i in range(length) if 0 <= i + by < length]
    return lax.ppermute(value, axis, pairs)


def turning(numbers, period, direction):
    angles = direction * full_turn / period * (numbers % period).astype(np.float64)
    return (jnp.asarray(np.cos(angles), jnp.float32), jnp.asarray(np.sin(angles), jnp.float32))


def rotate(values, cosine, sine):
    return jnp.stack([values[0] * cosine - values[1] * sine, values[0] * sine + values[1] * cosine])


def times_complex(first, second):
    return jnp.stack(
        [first[0] * second[0] - first[1] * second[1], first[0] * second[1] + first[1] * second[0]]
    )


def conjugate(values):
    return jnp.stack([values[0], -values[1]])


def mix_axis(values, count, direction, pattern):
    index = np.arange(count, dtype=np.int64)
    angles = -full_turn / count * ((index[:, None] * index[None, :]) % count).astype(np.float64)
    cosine, sine = np.cos(angles), np.sin(angles)
    matrix = jnp.asarray(np.stack([np.stack([cosine, -sine]), np.stack([sine, cosine])]), jnp.float32)
    pair, result = pattern.split("->")
    table, operand = pair.split(",")
    order = "zy" if direction < 0 else "yz"
    joined = order + table + ",y" + operand + "->z" + result
    return jnp.einsum(joined, matrix, values, precision=transform_mode)


def grid_places(parts, length):
    return (
        np.arange(parts, dtype=np.int64)[:, None] * length
        + np.arange(length, dtype=np.int64)[None, :]
    )


def forward_padded(signal):
    parts = signal.shape[1]
    length = signal.shape[2]
    seq_total = parts * length
    cosine, sine = turning(grid_places(parts, length), 2 * seq_total, -1.0)
    values = jnp.stack(
        [jnp.stack([signal, signal * cosine]), jnp.stack([jnp.zeros_like(signal), signal * sine])]
    )
    values = mix_axis(values, parts, -1.0, "ap,hrpj->hraj")
    index_a = np.arange(parts, dtype=np.int64)[:, None]
    index_j = np.arange(length, dtype=np.int64)[None, :]
    cosine, sine = turning(index_a * index_j, seq_total, -1.0)
    values = rotate(values, cosine, sine)
    return mix_axis(values, length, -1.0, "bj,hraj->hrab")


def inverse_padded(spectrum):
    half = spectrum.shape[2] // 2
    first = spectrum[:, :, :half]
    second = spectrum[:, :, half:]
    joined = jnp.stack([first[0] - second[1], first[1] + second[0]])
    parts = spectrum.shape[3]
    length = spectrum.shape[4]
    seq_total = parts * length
    values = mix_axis(joined, length, 1.0, "jb,hrab->hraj")
    index_a = np.arange(parts, dtype=np.int64)[:, None]
    index_j = np.arange(length, dtype=np.int64)[None, :]
    cosine, sine = turning(index_a * index_j, seq_total, -1.0)
    values = jnp.stack(
        [values[0] * cosine + values[1] * sine, values[1] * cosine - values[0] * sine]
    )
    values = mix_axis(values, parts, 1.0, "pa,hraj->hrpj") / seq_total
    cosine, sine = turning(grid_places(parts, length), 2 * seq_total, -1.0)
    real_part = 0.5 * (values[0, 0] + values[0, 1] * cosine + values[1, 1] * sine)
    other_part = 0.5 * (values[1, 0] - values[0, 1] * sine + values[1, 1] * cosine)
    return jnp.concatenate([real_part, other_part], axis=0)


def to_channels(stacked):
    return lax.all_to_all(
        jnp.swapaxes(stacked, 1, 2)[:, :, None, :], "inner", split_axis=1, concat_axis=2, tiled=True
    )


def to_positions(values):
    moved = lax.all_to_all(values, "inner", split_axis=2, concat_axis=1, tiled=True)
    return jnp.swapaxes(moved[:, :, 0, :], 1, 2)


def filter_features(seq_total, bands):
    places = np.arange(seq_total, dtype=np.int64)
    columns = [places.astype(np.float32) / np.float32(seq_total)]
    for band in range(bands):
        stride = min(2**band, seq_total // 4)
        phases = places % (seq_total // stride) * stride
        angles = np.float32(full_turn / seq_total) * phases.astype(np.float32)
        columns.append(np.cos(angles))
        columns.append(np.sin(angles))
    return jnp.asarray(np.stack(columns, axis=0), jnp.float32)


def decay_window(rates, places):
    return jnp.exp(-rates * places.astype(jnp.float32)) * jnp.sqrt(-jnp.expm1(-2.0 * rates))


def split_wide(values):
    rounded = lax.reduce_precision(values, exponent_bits=8, mantissa_bits=7)
    return rounded.astype(jnp.bfloat16), (values - rounded).astype(jnp.bfloat16)


def body(projected, short_weight, filter_in, filter_bias, filter_out, filter_decay, cotangent):
    parts = lax.axis_size("inner")
    inner_id = lax.axis_index("inner")
    length = projected.shape[0]
    chans = projected.shape[2]
    taps = short_weight.shape[0]
    bands = (filter_in.shape[0] - 1) // 2
    seq_total = parts * length
    slices = chans // parts
    places = inner_id * length + jnp.arange(length, dtype=jnp.int32)
    activity = jnp.sin(
        jnp.dot(
            jnp.transpose(
                lax.dynamic_slice_in_dim(filter_features(seq_total, bands), inner_id * length, length, 1)
            ),
            filter_in,
            precision=exact_mode,
        )
        + filter_bias
    )
    shaped = jnp.dot(activity, filter_out, precision=exact_mode)
    long_filter = shaped * decay_window(filter_decay[None, :], places[:, None])
    filter_upper, filter_lower = split_wide(long_filter)
    outgoing = jnp.concatenate(
        [projected, cotangent[:, None], filter_upper[:, None], filter_lower[:, None]], axis=1
    )
    outgoing = lax.optimization_barrier(outgoing)
    arrived = lax.all_to_all(
        outgoing.reshape(length, 6, parts, slices), "inner", split_axis=2, concat_axis=0, tiled=True
    )
    moved = jnp.transpose(arrived.reshape(seq_total, 6, slices), (1, 2, 0))
    first = inner_id * slices
    weights = lax.dynamic_slice_in_dim(short_weight, first, slices, axis=2)[:, :, :, None]
    mixed = []
    for group in range(3):
        padded = jnp.pad(moved[group], ((0, 0), (taps - 1, 0)))
        total = jnp.zeros((slices, seq_total), jnp.float32)
        for offset in range(taps):
            total = total + weights[offset, group] * padded[
                :, taps - 1 - offset : taps - 1 - offset + seq_total
            ]
        mixed.append(total)
    query, key_part, value_part = mixed
    product = key_part * value_part
    grad_conv = moved[3] * query
    long_rows = moved[4].astype(jnp.float32) + moved[5].astype(jnp.float32)
    signal_rows = product.reshape(slices, parts, length)
    filter_rows = long_rows.reshape(slices, parts, length)
    grad_rows = grad_conv.reshape(slices, parts, length)
    spectra = forward_padded(jnp.concatenate([signal_rows, filter_rows, grad_rows], axis=0))
    signal_spec = spectra[:, :, :slices]
    filter_spec = spectra[:, :, slices : 2 * slices]
    grad_spec = spectra[:, :, 2 * slices :]
    paired = jnp.concatenate(
        [
            times_complex(signal_spec, filter_spec),
            times_complex(conjugate(filter_spec), grad_spec),
            times_complex(grad_spec, conjugate(signal_spec)),
        ],
        axis=2,
    )
    spread = slices // 2
    ordered = jnp.concatenate(
        [paired[:, :, : slices], paired[:, :, 2 * slices : 2 * slices + spread],
         paired[:, :, slices : 2 * slices], paired[:, :, 2 * slices + spread :]],
        axis=2,
    )
    returned = inverse_padded(ordered)
    returned = jnp.concatenate(
        [returned[:slices], returned[slices + spread : 2 * slices + spread],
         returned[slices : slices + spread], returned[2 * slices + spread :]],
        axis=0,
    ).reshape(3, slices, seq_total)
    conv = returned[0]
    grad_product = returned[1]
    grad_filter = returned[2] / math.sqrt(seq_total)
    operator_out = (query * conv).astype(jnp.bfloat16)
    grad_mixed = [moved[3] * conv, grad_product * value_part, grad_product * key_part]
    grad_projected = []
    for group in range(3):
        padded = jnp.pad(grad_mixed[group], ((0, 0), (0, taps - 1)))
        total = jnp.zeros((slices, seq_total), jnp.float32)
        for offset in range(taps):
            total = total + weights[offset, group] * padded[:, offset : offset + seq_total]
        grad_projected.append(total.astype(jnp.bfloat16))
    grad_upper, grad_lower = split_wide(grad_filter)
    leaving = jnp.transpose(
        jnp.stack([operator_out] + grad_projected + [grad_upper, grad_lower]), (2, 0, 1)
    )
    back = lax.all_to_all(
        leaving.reshape(parts, length, 6, 1, slices), "inner", split_axis=0, concat_axis=3, tiled=True
    ).reshape(length, 6, chans)
    grad_out = back[:, 4].astype(jnp.float32) + back[:, 5].astype(jnp.float32)
    return (back[:, 0], back[:, 1:4], grad_out)


def solution(mesh):
    in_specs = (
        P("inner", None, "outer"),
        P(None, None, "outer"),
        P(),
        P(),
        P(None, "outer"),
        P("outer"),
        P("inner", "outer"),
    )
    out_specs = (P("inner", "outer"), P("inner", None, "outer"), P("inner", "outer"))
    return jax.shard_map(body, mesh=mesh, in_specs=in_specs, out_specs=out_specs, check_vma=False)
```

```python
import math

import jax
import numpy as np
import jax.numpy as jnp
from jax import lax
from jax.sharding import PartitionSpec as P

exact_mode = lax.Precision.HIGHEST
transform_mode = lax.Precision.HIGH
full_turn = 6.283185307179586


def passed_along(value, axis, by):
    length = lax.axis_size(axis)
    pairs = [(i, i + by) for i in range(length) if 0 <= i + by < length]
    return lax.ppermute(value, axis, pairs)


def turning(numbers, period, direction):
    angles = direction * full_turn / period * (numbers % period).astype(np.float64)
    return (jnp.asarray(np.cos(angles), jnp.float32), jnp.asarray(np.sin(angles), jnp.float32))


def rotate(values, cosine, sine):
    return jnp.stack([values[0] * cosine - values[1] * sine, values[0] * sine + values[1] * cosine])


def times_complex(first, second):
    return jnp.stack(
        [first[0] * second[0] - first[1] * second[1], first[0] * second[1] + first[1] * second[0]]
    )


def conjugate(values):
    return jnp.stack([values[0], -values[1]])


def block_matrix(count):
    index = np.arange(count, dtype=np.int64)
    angles = -full_turn / count * ((index[:, None] * index[None, :]) % count).astype(np.float64)
    cosine, sine = np.cos(angles), np.sin(angles)
    return jnp.asarray(np.stack([np.stack([cosine, -sine]), np.stack([sine, cosine])]), jnp.float32)


def transform_tables(parts, length):
    seq_total = parts * length
    index_a = np.arange(parts, dtype=np.int64)[:, None]
    index_j = np.arange(length, dtype=np.int64)[None, :]
    return {
        "small": block_matrix(parts),
        "large": block_matrix(length),
        "twist": turning(grid_places(parts, length), 2 * seq_total, -1.0),
        "spin": turning(index_a * index_j, seq_total, -1.0),
    }


def mix_axis(values, matrix, direction, pattern):
    pair, result = pattern.split("->")
    table, operand = pair.split(",")
    order = "zy" if direction < 0 else "yz"
    joined = order + table + ",y" + operand + "->z" + result
    return jnp.einsum(joined, matrix, values, precision=transform_mode)


def grid_places(parts, length):
    return (
        np.arange(parts, dtype=np.int64)[:, None] * length
        + np.arange(length, dtype=np.int64)[None, :]
    )


def forward_padded(signal, tables):
    parts = signal.shape[1]
    length = signal.shape[2]
    seq_total = parts * length
    cosine, sine = tables["twist"]
    values = jnp.stack(
        [jnp.stack([signal, signal * cosine]), jnp.stack([jnp.zeros_like(signal), signal * sine])]
    )
    values = mix_axis(values, tables["small"], -1.0, "ap,hrpj->hraj")
    index_a = np.arange(parts, dtype=np.int64)[:, None]
    index_j = np.arange(length, dtype=np.int64)[None, :]
    cosine, sine = tables["spin"]
    values = rotate(values, cosine, sine)
    return mix_axis(values, tables["large"], -1.0, "bj,hraj->hrab")


def inverse_padded(spectrum, tables):
    half = spectrum.shape[2] // 2
    first = spectrum[:, :, :half]
    second = spectrum[:, :, half:]
    joined = jnp.stack([first[0] - second[1], first[1] + second[0]])
    parts = spectrum.shape[3]
    length = spectrum.shape[4]
    seq_total = parts * length
    values = mix_axis(joined, tables["large"], 1.0, "jb,hrab->hraj")
    index_a = np.arange(parts, dtype=np.int64)[:, None]
    index_j = np.arange(length, dtype=np.int64)[None, :]
    cosine, sine = tables["spin"]
    values = jnp.stack(
        [values[0] * cosine + values[1] * sine, values[1] * cosine - values[0] * sine]
    )
    values = mix_axis(values, tables["small"], 1.0, "pa,hraj->hrpj") / seq_total
    cosine, sine = tables["twist"]
    real_part = 0.5 * (values[0, 0] + values[0, 1] * cosine + values[1, 1] * sine)
    other_part = 0.5 * (values[1, 0] - values[0, 1] * sine + values[1, 1] * cosine)
    return jnp.concatenate([real_part, other_part], axis=0)


def to_channels(stacked):
    return lax.all_to_all(
        jnp.swapaxes(stacked, 1, 2)[:, :, None, :], "inner", split_axis=1, concat_axis=2, tiled=True
    )


def to_positions(values):
    moved = lax.all_to_all(values, "inner", split_axis=2, concat_axis=1, tiled=True)
    return jnp.swapaxes(moved[:, :, 0, :], 1, 2)


def filter_features(seq_total, bands):
    places = np.arange(seq_total, dtype=np.int64)
    columns = [places.astype(np.float32) / np.float32(seq_total)]
    for band in range(bands):
        stride = min(2**band, seq_total // 4)
        phases = places % (seq_total // stride) * stride
        angles = np.float32(full_turn / seq_total) * phases.astype(np.float32)
        columns.append(np.cos(angles))
        columns.append(np.sin(angles))
    return jnp.asarray(np.stack(columns, axis=0), jnp.float32)


def decay_window(rates, places):
    return jnp.exp(-rates * places.astype(jnp.float32)) * jnp.sqrt(-jnp.expm1(-2.0 * rates))


def split_wide(values):
    rounded = lax.reduce_precision(values, exponent_bits=8, mantissa_bits=7)
    return rounded.astype(jnp.bfloat16), (values - rounded).astype(jnp.bfloat16)


def body(projected, short_weight, filter_in, filter_bias, filter_out, filter_decay, cotangent):
    parts = lax.axis_size("inner")
    inner_id = lax.axis_index("inner")
    length = projected.shape[0]
    chans = projected.shape[2]
    taps = short_weight.shape[0]
    bands = (filter_in.shape[0] - 1) // 2
    seq_total = parts * length
    slices = chans // parts
    places = inner_id * length + jnp.arange(length, dtype=jnp.int32)
    activity = jnp.sin(
        jnp.dot(
            jnp.transpose(
                lax.dynamic_slice_in_dim(filter_features(seq_total, bands), inner_id * length, length, 1)
            ),
            filter_in,
            precision=exact_mode,
        )
        + filter_bias
    )
    shaped = jnp.dot(activity, filter_out, precision=exact_mode)
    long_filter = shaped * decay_window(filter_decay[None, :], places[:, None])
    filter_upper, filter_lower = split_wide(long_filter)
    outgoing = jnp.concatenate(
        [projected, cotangent[:, None], filter_upper[:, None], filter_lower[:, None]], axis=1
    )
    outgoing, tables = lax.optimization_barrier((outgoing, transform_tables(parts, length)))
    arrived = lax.all_to_all(
        outgoing.reshape(length, 6, parts, slices), "inner", split_axis=2, concat_axis=0, tiled=True
    )
    moved = jnp.transpose(arrived.reshape(seq_total, 6, slices), (1, 2, 0))
    first = inner_id * slices
    weights = lax.dynamic_slice_in_dim(short_weight, first, slices, axis=2)[:, :, :, None]
    mixed = []
    for group in range(3):
        padded = jnp.pad(moved[group], ((0, 0), (taps - 1, 0)))
        total = jnp.zeros((slices, seq_total), jnp.float32)
        for offset in range(taps):
            total = total + weights[offset, group] * padded[
                :, taps - 1 - offset : taps - 1 - offset + seq_total
            ]
        mixed.append(total)
    query, key_part, value_part = mixed
    product = key_part * value_part
    grad_conv = moved[3] * query
    long_rows = moved[4].astype(jnp.float32) + moved[5].astype(jnp.float32)
    signal_rows = product.reshape(slices, parts, length)
    filter_rows = long_rows.reshape(slices, parts, length)
    grad_rows = grad_conv.reshape(slices, parts, length)
    spectra = forward_padded(jnp.concatenate([signal_rows, filter_rows, grad_rows], axis=0), tables)
    signal_spec = spectra[:, :, :slices]
    filter_spec = spectra[:, :, slices : 2 * slices]
    grad_spec = spectra[:, :, 2 * slices :]
    paired = jnp.concatenate(
        [
            times_complex(signal_spec, filter_spec),
            times_complex(conjugate(filter_spec), grad_spec),
            times_complex(grad_spec, conjugate(signal_spec)),
        ],
        axis=2,
    )
    spread = slices // 2
    ordered = jnp.concatenate(
        [paired[:, :, : slices], paired[:, :, 2 * slices : 2 * slices + spread],
         paired[:, :, slices : 2 * slices], paired[:, :, 2 * slices + spread :]],
        axis=2,
    )
    returned = inverse_padded(ordered, tables)
    returned = jnp.concatenate(
        [returned[:slices], returned[slices + spread : 2 * slices + spread],
         returned[slices : slices + spread], returned[2 * slices + spread :]],
        axis=0,
    ).reshape(3, slices, seq_total)
    conv = returned[0]
    grad_product = returned[1]
    grad_filter = returned[2] / math.sqrt(seq_total)
    operator_out = (query * conv).astype(jnp.bfloat16)
    grad_mixed = [moved[3] * conv, grad_product * value_part, grad_product * key_part]
    grad_projected = []
    for group in range(3):
        padded = jnp.pad(grad_mixed[group], ((0, 0), (0, taps - 1)))
        total = jnp.zeros((slices, seq_total), jnp.float32)
        for offset in range(taps):
            total = total + weights[offset, group] * padded[:, offset : offset + seq_total]
        grad_projected.append(total.astype(jnp.bfloat16))
    grad_upper, grad_lower = split_wide(grad_filter)
    leaving = jnp.transpose(
        jnp.stack([operator_out] + grad_projected + [grad_upper, grad_lower]), (2, 0, 1)
    )
    back = lax.all_to_all(
        leaving.reshape(parts, length, 6, 1, slices), "inner", split_axis=0, concat_axis=3, tiled=True
    ).reshape(length, 6, chans)
    grad_out = back[:, 4].astype(jnp.float32) + back[:, 5].astype(jnp.float32)
    return (back[:, 0], back[:, 1:4], grad_out)


def solution(mesh):
    in_specs = (
        P("inner", None, "outer"),
        P(None, None, "outer"),
        P(),
        P(),
        P(None, "outer"),
        P("outer"),
        P("inner", "outer"),
    )
    out_specs = (P("inner", "outer"), P("inner", None, "outer"), P("inner", "outer"))
    return jax.shard_map(body, mesh=mesh, in_specs=in_specs, out_specs=out_specs, check_vma=False)
```

```python
import math

import jax
import numpy as np
import jax.numpy as jnp
from jax import lax
from jax.sharding import PartitionSpec as P

exact_mode = lax.Precision.HIGHEST
transform_mode = lax.Precision.HIGH
full_turn = 6.283185307179586


def passed_along(value, axis, by):
    length = lax.axis_size(axis)
    pairs = [(i, i + by) for i in range(length) if 0 <= i + by < length]
    return lax.ppermute(value, axis, pairs)


def turning(numbers, period, direction):
    angles = direction * full_turn / period * (numbers % period).astype(np.float64)
    return (jnp.asarray(np.cos(angles), jnp.float32), jnp.asarray(np.sin(angles), jnp.float32))


def rotate(values, cosine, sine):
    return jnp.stack([values[0] * cosine - values[1] * sine, values[0] * sine + values[1] * cosine])


def times_complex(first, second):
    return jnp.stack(
        [first[0] * second[0] - first[1] * second[1], first[0] * second[1] + first[1] * second[0]]
    )


def conjugate(values):
    return jnp.stack([values[0], -values[1]])


def block_matrix(count):
    index = np.arange(count, dtype=np.int64)
    angles = -full_turn / count * ((index[:, None] * index[None, :]) % count).astype(np.float64)
    return jnp.asarray(np.stack([np.cos(angles), np.sin(angles)]), jnp.float32)


def joined_matrix(parts):
    return jnp.stack([jnp.stack([parts[0], -parts[1]]), jnp.stack([parts[1], parts[0]])])


def transform_tables(parts, length):
    seq_total = parts * length
    index_a = np.arange(parts, dtype=np.int64)[:, None]
    index_j = np.arange(length, dtype=np.int64)[None, :]
    return {
        "small": block_matrix(parts),
        "large": block_matrix(length),
        "twist": turning(grid_places(parts, length), 2 * seq_total, -1.0),
        "spin": turning(index_a * index_j, seq_total, -1.0),
    }


def mix_axis(values, matrix, direction, pattern):
    pair, result = pattern.split("->")
    table, operand = pair.split(",")
    order = "zy" if direction < 0 else "yz"
    joined = order + table + ",y" + operand + "->z" + result
    return jnp.einsum(joined, matrix, values, precision=transform_mode)


def grid_places(parts, length):
    return (
        np.arange(parts, dtype=np.int64)[:, None] * length
        + np.arange(length, dtype=np.int64)[None, :]
    )


def forward_padded(signal, tables):
    parts = signal.shape[1]
    length = signal.shape[2]
    seq_total = parts * length
    cosine, sine = tables["twist"]
    values = jnp.stack(
        [jnp.stack([signal, signal * cosine]), jnp.stack([jnp.zeros_like(signal), signal * sine])]
    )
    values = mix_axis(values, tables["small"], -1.0, "ap,hrpj->hraj")
    index_a = np.arange(parts, dtype=np.int64)[:, None]
    index_j = np.arange(length, dtype=np.int64)[None, :]
    cosine, sine = tables["spin"]
    values = rotate(values, cosine, sine)
    return mix_axis(values, tables["large"], -1.0, "bj,hraj->hrab")


def inverse_padded(spectrum, tables):
    half = spectrum.shape[2] // 2
    first = spectrum[:, :, :half]
    second = spectrum[:, :, half:]
    joined = jnp.stack([first[0] - second[1], first[1] + second[0]])
    parts = spectrum.shape[3]
    length = spectrum.shape[4]
    seq_total = parts * length
    values = mix_axis(joined, tables["large"], 1.0, "jb,hrab->hraj")
    index_a = np.arange(parts, dtype=np.int64)[:, None]
    index_j = np.arange(length, dtype=np.int64)[None, :]
    cosine, sine = tables["spin"]
    values = jnp.stack(
        [values[0] * cosine + values[1] * sine, values[1] * cosine - values[0] * sine]
    )
    values = mix_axis(values, tables["small"], 1.0, "pa,hraj->hrpj") / seq_total
    cosine, sine = tables["twist"]
    real_part = 0.5 * (values[0, 0] + values[0, 1] * cosine + values[1, 1] * sine)
    other_part = 0.5 * (values[1, 0] - values[0, 1] * sine + values[1, 1] * cosine)
    return jnp.concatenate([real_part, other_part], axis=0)


def to_channels(stacked):
    return lax.all_to_all(
        jnp.swapaxes(stacked, 1, 2)[:, :, None, :], "inner", split_axis=1, concat_axis=2, tiled=True
    )


def to_positions(values):
    moved = lax.all_to_all(values, "inner", split_axis=2, concat_axis=1, tiled=True)
    return jnp.swapaxes(moved[:, :, 0, :], 1, 2)


def filter_features(seq_total, bands):
    places = np.arange(seq_total, dtype=np.int64)
    columns = [places.astype(np.float32) / np.float32(seq_total)]
    for band in range(bands):
        stride = min(2**band, seq_total // 4)
        phases = places % (seq_total // stride) * stride
        angles = np.float32(full_turn / seq_total) * phases.astype(np.float32)
        columns.append(np.cos(angles))
        columns.append(np.sin(angles))
    return jnp.asarray(np.stack(columns, axis=0), jnp.float32)


def decay_window(rates, places):
    return jnp.exp(-rates * places.astype(jnp.float32)) * jnp.sqrt(-jnp.expm1(-2.0 * rates))


def split_wide(values):
    rounded = lax.reduce_precision(values, exponent_bits=8, mantissa_bits=7)
    return rounded.astype(jnp.bfloat16), (values - rounded).astype(jnp.bfloat16)


def body(projected, short_weight, filter_in, filter_bias, filter_out, filter_decay, cotangent):
    parts = lax.axis_size("inner")
    inner_id = lax.axis_index("inner")
    length = projected.shape[0]
    chans = projected.shape[2]
    taps = short_weight.shape[0]
    bands = (filter_in.shape[0] - 1) // 2
    seq_total = parts * length
    slices = chans // parts
    places = inner_id * length + jnp.arange(length, dtype=jnp.int32)
    activity = jnp.sin(
        jnp.dot(
            jnp.transpose(
                lax.dynamic_slice_in_dim(filter_features(seq_total, bands), inner_id * length, length, 1)
            ),
            filter_in,
            precision=exact_mode,
        )
        + filter_bias
    )
    shaped = jnp.dot(activity, filter_out, precision=exact_mode)
    long_filter = shaped * decay_window(filter_decay[None, :], places[:, None])
    filter_upper, filter_lower = split_wide(long_filter)
    outgoing = jnp.concatenate(
        [projected, cotangent[:, None], filter_upper[:, None], filter_lower[:, None]], axis=1
    )
    outgoing, tables = lax.optimization_barrier((outgoing, transform_tables(parts, length)))
    tables["small"] = joined_matrix(tables["small"])
    tables["large"] = joined_matrix(tables["large"])
    arrived = lax.all_to_all(
        outgoing.reshape(length, 6, parts, slices), "inner", split_axis=2, concat_axis=0, tiled=True
    )
    moved = jnp.transpose(arrived.reshape(seq_total, 6, slices), (1, 2, 0))
    first = inner_id * slices
    weights = lax.dynamic_slice_in_dim(short_weight, first, slices, axis=2)[:, :, :, None]
    mixed = []
    for group in range(3):
        padded = jnp.pad(moved[group], ((0, 0), (taps - 1, 0)))
        total = jnp.zeros((slices, seq_total), jnp.float32)
        for offset in range(taps):
            total = total + weights[offset, group] * padded[
                :, taps - 1 - offset : taps - 1 - offset + seq_total
            ]
        mixed.append(total)
    query, key_part, value_part = mixed
    product = key_part * value_part
    grad_conv = moved[3] * query
    long_rows = moved[4].astype(jnp.float32) + moved[5].astype(jnp.float32)
    signal_rows = product.reshape(slices, parts, length)
    filter_rows = long_rows.reshape(slices, parts, length)
    grad_rows = grad_conv.reshape(slices, parts, length)
    spectra = forward_padded(jnp.concatenate([signal_rows, filter_rows, grad_rows], axis=0), tables)
    signal_spec = spectra[:, :, :slices]
    filter_spec = spectra[:, :, slices : 2 * slices]
    grad_spec = spectra[:, :, 2 * slices :]
    paired = jnp.concatenate(
        [
            times_complex(signal_spec, filter_spec),
            times_complex(conjugate(filter_spec), grad_spec),
            times_complex(grad_spec, conjugate(signal_spec)),
        ],
        axis=2,
    )
    spread = slices // 2
    ordered = jnp.concatenate(
        [paired[:, :, : slices], paired[:, :, 2 * slices : 2 * slices + spread],
         paired[:, :, slices : 2 * slices], paired[:, :, 2 * slices + spread :]],
        axis=2,
    )
    returned = inverse_padded(ordered, tables)
    returned = jnp.concatenate(
        [returned[:slices], returned[slices + spread : 2 * slices + spread],
         returned[slices : slices + spread], returned[2 * slices + spread :]],
        axis=0,
    ).reshape(3, slices, seq_total)
    conv = returned[0]
    grad_product = returned[1]
    grad_filter = returned[2] / math.sqrt(seq_total)
    operator_out = (query * conv).astype(jnp.bfloat16)
    grad_mixed = [moved[3] * conv, grad_product * value_part, grad_product * key_part]
    grad_projected = []
    for group in range(3):
        padded = jnp.pad(grad_mixed[group], ((0, 0), (0, taps - 1)))
        total = jnp.zeros((slices, seq_total), jnp.float32)
        for offset in range(taps):
            total = total + weights[offset, group] * padded[:, offset : offset + seq_total]
        grad_projected.append(total.astype(jnp.bfloat16))
    grad_upper, grad_lower = split_wide(grad_filter)
    leaving = jnp.transpose(
        jnp.stack([operator_out] + grad_projected + [grad_upper, grad_lower]), (2, 0, 1)
    )
    back = lax.all_to_all(
        leaving.reshape(parts, length, 6, 1, slices), "inner", split_axis=0, concat_axis=3, tiled=True
    ).reshape(length, 6, chans)
    grad_out = back[:, 4].astype(jnp.float32) + back[:, 5].astype(jnp.float32)
    return (back[:, 0], back[:, 1:4], grad_out)


def solution(mesh):
    in_specs = (
        P("inner", None, "outer"),
        P(None, None, "outer"),
        P(),
        P(),
        P(None, "outer"),
        P("outer"),
        P("inner", "outer"),
    )
    out_specs = (P("inner", "outer"), P("inner", None, "outer"), P("inner", "outer"))
    return jax.shard_map(body, mesh=mesh, in_specs=in_specs, out_specs=out_specs, check_vma=False)
```
